128 devices in a mesh: wide: 16 (over y_hi, z, core), blk: 8 (over x, y_lo).
Axes of the slice: x: 4, y: 4 (y_hi: 2, y_lo: 2; y = y_hi * 2 + y_lo), z: 4, core: 2. Of those that a mesh axis runs over, the one named last changes fastest.
Arguments:
- queries: bfloat16 [512, 64, 512], P(('wide', 'blk')), may hold values from -6 to 6
- references: bfloat16 [256, 64, 512], P(('wide', 'blk')), may hold values from -6 to 6
- query_taps: bfloat16 [16, 9], replicated, may hold values from -2 to 2
- ref_taps: bfloat16 [16, 9], replicated, may hold values from -0.5 to 0.5
- tap_bias: float32 [16], replicated, may hold values from -3 to 3
- candidates: int32 [128, 16], P(('wide', 'blk')), may hold values 0 or 1
Outputs:
- scores: float32 [512, 256], P(('wide', 'blk'))
The draws below stay inside these ranges and needn't reach their ends.
All inputs are finite; a program needn't handle non-finite values. No bound on the sum of `candidates` on one device may be relied on, other than what follows from the above.
Results may differ from the reference program's by a relative error of at most 0.0006.
Values may be sent and summed in bfloat16 or wider, within the bound.
No kernel may reach another device: no remote copies, remote signals or barrier semaphores. Data moves between devices by JAX's collectives and lax.ppermute only.
A program may use at most 64 MiB of HBM per device.

```python
import math
import jax
import jax.numpy as jnp
from jax import lax

SIDE = 8
C = 512
HID = 16
QT = 4
CELLS = 64
TILES = 128
BLOCKS = 16
BR = 16
NQ = 512
NR = 256


def plant(values, own_key, low, high):
    place = [jax.random.randint(jax.random.fold_in(own_key, axis), (), 0, length) for axis, length in enumerate(values.shape)]
    main_axis = values.shape.index(max(values.shape))
    neighbour = place[:main_axis] + [(place[main_axis] + 1) % values.shape[main_axis]] + place[main_axis + 1:]
    return values.at[tuple(place)].set(low).at[tuple(neighbour)].set(high)


def levels(key, shape, split, least, high):
    loudness = 1.0
    for axis_at, shards_of in split:
        steps = jax.random.uniform(jax.random.fold_in(jax.random.fold_in(key, 6), axis_at), (shards_of,), jnp.float32, least / len(split), high / len(split))
        loudness = loudness * jnp.repeat(jnp.exp(steps), shape[axis_at] // shards_of).reshape((-1,) + (1,) * (len(shape) - 1 - axis_at))
    return loudness


def bell_draw(own_key, dims, deviation, limit, split=(), held_as=jnp.bfloat16):
    values = deviation * jax.random.normal(own_key, dims, jnp.float32)
    if split:
        values = values * levels(own_key, dims, split, -0.22, 0.18)
    return jnp.clip(values, -limit, limit).astype(held_as)


def setup_inputs(seed: int = 0) -> dict:
    key_of = jax.random.split(jax.random.key(seed), 7)
    queries = bell_draw(key_of[0], (NQ, CELLS, C), 1.0, 6.0, ((0, 128),))
    references = bell_draw(key_of[1], (NR, CELLS, C), 1.0, 6.0, ((0, 128),))
    query_taps = bell_draw(key_of[2], (HID, 9), 9 ** -0.5, 2.0)
    ref_taps = bell_draw(key_of[3], (HID, 9), (9 * HID) ** -0.5, 0.5)
    tap_bias = bell_draw(key_of[4], (HID,), 0.5, 3.0, (), jnp.float32)
    candidates = plant((jax.random.randint(key_of[5], (TILES, BLOCKS), 0, 2) < 1).astype(jnp.int32), jax.random.fold_in(key_of[5], 1), 0, 1)
    return {"queries": queries, "references": references, "query_taps": query_taps, "ref_taps": ref_taps, "tap_bias": tap_bias, "candidates": candidates}


epsilon = 1e-06

def conv_table(weights, width):
    count = width * width
    position = jnp.arange(count, dtype=jnp.int32)
    grid_row = position // width
    grid_col = position % width
    delta_row = grid_row[None, :] - grid_row[:, None]
    delta_col = grid_col[None, :] - grid_col[:, None]
    inside = (jnp.abs(delta_row) <= 1) & (jnp.abs(delta_col) <= 1)
    tap_index = (delta_row + 1) * 3 + (delta_col + 1)
    selector = (tap_index[None] == jnp.arange(9, dtype=jnp.int32)[:, None, None]) & inside[None]
    table = lax.optimization_barrier(jnp.sum(jnp.where(selector[None], weights.astype(jnp.float32)[:, :, None, None], jnp.float32(0.0)), axis=1))
    return table.astype(jnp.bfloat16)

def normalize(features):
    values = features.astype(jnp.float32)
    inverse_rms = lax.rsqrt(lax.optimization_barrier(jnp.mean(values * values, axis=-1, keepdims=True)) + epsilon)
    return (values * inverse_rms).astype(jnp.bfloat16)

def pair_scores(query_unit, ref_unit, query_table, ref_table, tap_bias):
    count = query_unit.shape[0]
    others = ref_unit.shape[0]
    cell_count = query_unit.shape[1]
    depth = query_unit.shape[2]
    correlation = jnp.dot(query_unit.reshape(count * cell_count, depth), ref_unit.reshape(others * cell_count, depth).T, preferred_element_type=jnp.float32)
    correlation = (correlation / math.sqrt(depth)).astype(jnp.bfloat16).reshape(count, cell_count, others, cell_count)
    hidden = jnp.einsum('kai,pirj->pkarj', query_table.astype(jnp.float32), correlation.astype(jnp.float32))
    hidden = jnp.maximum(hidden + tap_bias[None, :, None, None, None], 0.0).astype(jnp.bfloat16)
    filtered = jnp.einsum('pkarj,kbj->parb', hidden.astype(jnp.float32), ref_table.astype(jnp.float32))
    row_pool = lax.optimization_barrier(jnp.mean(lax.optimization_barrier(jnp.max(filtered, axis=3)), axis=1))
    col_pool = lax.optimization_barrier(jnp.mean(lax.optimization_barrier(jnp.max(filtered, axis=1)), axis=2))
    return 0.5 * (row_pool + col_pool)

def reference(queries, references, query_taps, ref_taps, tap_bias, candidates):
    query_table = conv_table(query_taps, SIDE)
    ref_table = conv_table(ref_taps, SIDE)
    query_unit = normalize(queries).reshape(TILES, QT, CELLS, C)
    ref_unit = normalize(references).reshape(BLOCKS, BR, CELLS, C)

    def per_tile(query_tile):

        def per_block(ref_block):
            return pair_scores(query_tile, ref_block, query_table, ref_table, tap_bias)
        return lax.map(per_block, ref_unit)
    scores = lax.map(per_tile, query_unit)
    scores = jnp.transpose(scores, (0, 2, 1, 3))
    keep = candidates[:, None, :, None] != 0
    return jnp.where(keep, scores, jnp.float32(0.0)).reshape(NQ, NR).astype(jnp.float32)
```

```python
import math

import jax
import jax.numpy as jnp
from jax import lax
from jax.experimental import pallas as pl
from jax.experimental.pallas import tpu as pltpu
from jax.sharding import PartitionSpec as P

SIDE = 8


epsilon = 1e-06


def conv_table(weights, width):
    count = width * width
    position = jnp.arange(count, dtype=jnp.int32)
    grid_row = position // width
    grid_col = position % width
    delta_row = grid_row[None, :] - grid_row[:, None]
    delta_col = grid_col[None, :] - grid_col[:, None]
    inside = (jnp.abs(delta_row) <= 1) & (jnp.abs(delta_col) <= 1)
    tap_index = (delta_row + 1) * 3 + (delta_col + 1)
    selector = (tap_index[None] == jnp.arange(9, dtype=jnp.int32)[:, None, None]) & inside[None]
    table = jnp.sum(
        jnp.where(selector[None], weights.astype(jnp.float32)[:, :, None, None], jnp.float32(0.0)),
        axis=1,
    )
    return table.astype(jnp.bfloat16)


def normalize(features):
    values = features.astype(jnp.float32)
    inverse_rms = lax.rsqrt(jnp.mean(values * values, axis=-1, keepdims=True) + epsilon)
    return (values * inverse_rms).astype(jnp.bfloat16)


CH = 256


def filter_kernel(q_ref, r_ref, qt_ref, bias_ref, rt_ref, col_ref, row_ref, c_scr, h_scr):
    rows = q_ref.shape[0]
    lanes = r_ref.shape[0]
    chunks = lanes // CH
    hid = rt_ref.shape[0]
    cells = qt_ref.shape[1]
    depth = q_ref.shape[1]
    scale = math.sqrt(depth)
    qt = q_ref[...]
    for rc in range(chunks):
        corr = lax.dot_general(
            qt, r_ref[rc * CH:(rc + 1) * CH, :], (((1,), (1,)), ((), ())),
            preferred_element_type=jnp.float32,
        )
        c_scr[:, rc * CH:(rc + 1) * CH] = (corr / scale).astype(jnp.bfloat16)

    def per_query(p, carry):
        base = pl.multiple_of(p * cells, cells)
        for rc in range(chunks):
            cc = c_scr[pl.ds(base, cells), rc * CH:(rc + 1) * CH]
            for kg in range(hid // 4):
                hq = jnp.dot(
                    qt_ref[kg * 4 * cells:(kg + 1) * 4 * cells, :], cc,
                    preferred_element_type=jnp.float32,
                )
                hq = jnp.maximum(hq + bias_ref[kg * 4 * cells:(kg + 1) * 4 * cells, :], 0.0)
                hq = hq.astype(jnp.bfloat16)
                for kk in range(4):
                    k = kg * 4 + kk
                    h_scr[k, rc * cells:(rc + 1) * cells, :] = hq[kk * cells:(kk + 1) * cells, :]
        acc = jnp.dot(h_scr[0], rt_ref[0], preferred_element_type=jnp.float32)
        for k in range(1, hid):
            acc = acc + jnp.dot(h_scr[k], rt_ref[k], preferred_element_type=jnp.float32)
        col_ref[0, p] = jnp.max(acc.reshape(chunks, cells, CH), axis=1)
        accT = acc.T
        row_ref[0, p] = jnp.max(accT.reshape(CH // cells, cells, chunks * cells), axis=1)
        return carry

    lax.fori_loop(0, rows // cells, per_query, 0)


def local_scores(q_all, r_all, query_table, ref_table, tap_bias):
    nql, cells, depth = q_all.shape
    nrl = r_all.shape[0]
    hid = query_table.shape[0]
    qt_per = 4
    tiles = nql // qt_per
    chunks = nrl * cells // CH
    r4 = CH // cells
    qstack = query_table.reshape(hid * cells, cells)
    bias_col = jnp.repeat(tap_bias.astype(jnp.float32), cells)[:, None]
    eye = jnp.eye(r4, dtype=jnp.float32)
    rtT = jnp.transpose(ref_table.astype(jnp.float32), (0, 2, 1))
    rt = jnp.einsum("xy,kjb->kxjyb", eye, rtT).reshape(hid, CH, CH).astype(jnp.bfloat16)
    q2 = q_all.reshape(nql * cells, depth)
    r2 = r_all.reshape(nrl * cells, depth)
    col, row = pl.pallas_call(
        filter_kernel,
        grid=(tiles,),
        in_specs=[
            pl.BlockSpec((qt_per * cells, depth), lambda t: (t, 0)),
            pl.BlockSpec((nrl * cells, depth), lambda t: (0, 0)),
            pl.BlockSpec((hid * cells, cells), lambda t: (0, 0)),
            pl.BlockSpec((hid * cells, 1), lambda t: (0, 0)),
            pl.BlockSpec((hid, CH, CH), lambda t: (0, 0, 0)),
        ],
        out_specs=[
            pl.BlockSpec((1, qt_per, chunks, CH), lambda t: (t, 0, 0, 0)),
            pl.BlockSpec((1, qt_per, r4, chunks * cells), lambda t: (t, 0, 0, 0)),
        ],
        out_shape=[
            jax.ShapeDtypeStruct((tiles, qt_per, chunks, CH), jnp.float32),
            jax.ShapeDtypeStruct((tiles, qt_per, r4, chunks * cells), jnp.float32),
        ],
        scratch_shapes=[
            pltpu.VMEM((qt_per * cells, nrl * cells), jnp.bfloat16),
            pltpu.VMEM((hid, chunks * cells, CH), jnp.bfloat16),
        ],
        compiler_params=pltpu.CompilerParams(vmem_limit_bytes=48 * 1024 * 1024),
    )(q2, r2, qstack, bias_col, rt)
    col_pool = jnp.mean(col.reshape(tiles, qt_per, chunks, r4, cells), axis=-1)
    row_pool = jnp.mean(row.reshape(tiles, qt_per, r4, chunks, cells), axis=-1)
    row_pool = jnp.transpose(row_pool, (0, 1, 3, 2))
    return (0.5 * (row_pool + col_pool)).reshape(nql, nrl)


def shards(queries, references, query_taps, ref_taps, tap_bias, candidates):
    query_table = conv_table(query_taps, SIDE)
    ref_table = conv_table(ref_taps, SIDE)
    query_unit = normalize(queries)
    ref_unit = normalize(references)
    blk = lax.axis_size("blk")
    wide = lax.axis_size("wide")
    qt_per = query_unit.shape[0]
    rl = ref_unit.shape[0]
    q_all = lax.all_gather(query_unit, "blk", axis=0, tiled=True)
    r_all = lax.all_gather(ref_unit, "wide", axis=0, tiled=True)
    s = local_scores(q_all, r_all, query_table, ref_table, tap_bias)
    gathered = lax.all_gather(s, "blk", axis=0, tiled=False)
    me = lax.axis_index("blk")
    mine = lax.dynamic_slice_in_dim(gathered, me * qt_per, qt_per, axis=1)
    mine = mine.reshape(blk, qt_per, wide, rl)
    mine = jnp.transpose(mine, (1, 2, 0, 3)).reshape(qt_per, wide * blk * rl)
    block_refs = blk * rl
    keep = jnp.repeat(candidates[0] != 0, block_refs)
    return jnp.where(keep[None, :], mine, jnp.float32(0.0))


def solution(mesh):
    placed = (
        P(("wide", "blk"), None, None),
        P(("wide", "blk"), None, None),
        P(),
        P(),
        P(),
        P(("wide", "blk"), None),
    )
    return jax.shard_map(
        shards, mesh=mesh, in_specs=placed, out_specs=P(("wide", "blk"), None), check_vma=False
    )
```

```python
import math

import jax
import jax.numpy as jnp
from jax import lax
from jax.experimental import pallas as pl
from jax.experimental.pallas import tpu as pltpu
from jax.sharding import PartitionSpec as P

SIDE = 8


epsilon = 1e-06


def conv_table(weights, width):
    count = width * width
    position = jnp.arange(count, dtype=jnp.int32)
    grid_row = position // width
    grid_col = position % width
    delta_row = grid_row[None, :] - grid_row[:, None]
    delta_col = grid_col[None, :] - grid_col[:, None]
    inside = (jnp.abs(delta_row) <= 1) & (jnp.abs(delta_col) <= 1)
    tap_index = (delta_row + 1) * 3 + (delta_col + 1)
    selector = (tap_index[None] == jnp.arange(9, dtype=jnp.int32)[:, None, None]) & inside[None]
    table = jnp.sum(
        jnp.where(selector[None], weights.astype(jnp.float32)[:, :, None, None], jnp.float32(0.0)),
        axis=1,
    )
    return table.astype(jnp.bfloat16)


def normalize(features):
    values = features.astype(jnp.float32)
    inverse_rms = lax.rsqrt(jnp.mean(values * values, axis=-1, keepdims=True) + epsilon)
    return (values * inverse_rms).astype(jnp.bfloat16)


CH = 256


def filter_kernel(q_ref, r_ref, qt_ref, bias_ref, rtt_ref, col_ref, row_ref, c_scr, h_scr, rt_ref):
    rows = q_ref.shape[0]
    lanes = r_ref.shape[0]
    chunks = lanes // CH
    hid = rt_ref.shape[0]
    cells = qt_ref.shape[1]
    depth = q_ref.shape[1]
    scale = math.sqrt(depth)

    @pl.when(pl.program_id(0) == 0)
    def _():
        rt_ref[...] = jnp.zeros(rt_ref.shape, rt_ref.dtype)
        for k in range(hid):
            blockk = rtt_ref[k]
            for x in range(CH // cells):
                rt_ref[k, x * cells:(x + 1) * cells, x * cells:(x + 1) * cells] = blockk
    qt = q_ref[...]
    for rc in range(chunks):
        corr = lax.dot_general(
            qt, r_ref[rc * CH:(rc + 1) * CH, :], (((1,), (1,)), ((), ())),
            preferred_element_type=jnp.float32,
        )
        c_scr[:, rc * CH:(rc + 1) * CH] = (corr / scale).astype(jnp.bfloat16)

    def per_query(p, carry):
        base = pl.multiple_of(p * cells, cells)
        for rc in range(chunks):
            cc = c_scr[pl.ds(base, cells), rc * CH:(rc + 1) * CH]
            for kg in range(hid // 4):
                hq = jnp.dot(
                    qt_ref[kg * 4 * cells:(kg + 1) * 4 * cells, :], cc,
                    preferred_element_type=jnp.float32,
                )
                hq = jnp.maximum(hq + bias_ref[kg * 4 * cells:(kg + 1) * 4 * cells, :], 0.0)
                hq = hq.astype(jnp.bfloat16)
                for kk in range(4):
                    k = kg * 4 + kk
                    h_scr[k, rc * cells:(rc + 1) * cells, :] = hq[kk * cells:(kk + 1) * cells, :]
        acc = jnp.dot(h_scr[0], rt_ref[0], preferred_element_type=jnp.float32)
        for k in range(1, hid):
            acc = acc + jnp.dot(h_scr[k], rt_ref[k], preferred_element_type=jnp.float32)
        col_ref[0, p] = jnp.max(acc.reshape(chunks, cells, CH), axis=1)
        accT = acc.T
        row_ref[0, p] = jnp.max(accT.reshape(CH // cells, cells, chunks * cells), axis=1)
        return carry

    lax.fori_loop(0, rows // cells, per_query, 0)


def local_scores(q_all, r_all, query_table, ref_table, tap_bias):
    nql, cells, depth = q_all.shape
    nrl = r_all.shape[0]
    hid = query_table.shape[0]
    qt_per = 4
    tiles = nql // qt_per
    chunks = nrl * cells // CH
    r4 = CH // cells
    qstack = query_table.reshape(hid * cells, cells)
    bias_col = jnp.repeat(tap_bias.astype(jnp.float32), cells)[:, None]
    rtT = jnp.transpose(ref_table, (0, 2, 1))
    q2 = q_all.reshape(nql * cells, depth)
    r2 = r_all.reshape(nrl * cells, depth)
    col, row = pl.pallas_call(
        filter_kernel,
        grid=(tiles,),
        in_specs=[
            pl.BlockSpec((qt_per * cells, depth), lambda t: (t, 0)),
            pl.BlockSpec((nrl * cells, depth), lambda t: (0, 0)),
            pl.BlockSpec((hid * cells, cells), lambda t: (0, 0)),
            pl.BlockSpec((hid * cells, 1), lambda t: (0, 0)),
            pl.BlockSpec((hid, cells, cells), lambda t: (0, 0, 0)),
        ],
        out_specs=[
            pl.BlockSpec((1, qt_per, chunks, CH), lambda t: (t, 0, 0, 0)),
            pl.BlockSpec((1, qt_per, r4, chunks * cells), lambda t: (t, 0, 0, 0)),
        ],
        out_shape=[
            jax.ShapeDtypeStruct((tiles, qt_per, chunks, CH), jnp.float32),
            jax.ShapeDtypeStruct((tiles, qt_per, r4, chunks * cells), jnp.float32),
        ],
        scratch_shapes=[
            pltpu.VMEM((qt_per * cells, nrl * cells), jnp.bfloat16),
            pltpu.VMEM((hid, chunks * cells, CH), jnp.bfloat16),
            pltpu.VMEM((hid, CH, CH), jnp.bfloat16),
        ],
        compiler_params=pltpu.CompilerParams(vmem_limit_bytes=48 * 1024 * 1024),
    )(q2, r2, qstack, bias_col, rtT)
    col_pool = jnp.mean(col.reshape(tiles, qt_per, chunks, r4, cells), axis=-1)
    row_pool = jnp.mean(row.reshape(tiles, qt_per, r4, chunks, cells), axis=-1)
    row_pool = jnp.transpose(row_pool, (0, 1, 3, 2))
    return (0.5 * (row_pool + col_pool)).reshape(nql, nrl)


def shards(queries, references, query_taps, ref_taps, tap_bias, candidates):
    query_table = conv_table(query_taps, SIDE)
    ref_table = conv_table(ref_taps, SIDE)
    query_unit = normalize(queries)
    ref_unit = normalize(references)
    blk = lax.axis_size("blk")
    wide = lax.axis_size("wide")
    qt_per = query_unit.shape[0]
    rl = ref_unit.shape[0]
    q_all = lax.all_gather(query_unit, "blk", axis=0, tiled=True)
    parts = []
    for slot in range(rl):
        r_slot = lax.all_gather(ref_unit[slot:slot + 1], "wide", axis=0, tiled=True)
        parts.append(local_scores(q_all, r_slot, query_table, ref_table, tap_bias))
    s = jnp.stack(parts, axis=-1).reshape(blk, qt_per, wide, rl)
    me = lax.axis_index("blk")
    pieces = [lax.dynamic_index_in_dim(s, me, axis=0, keepdims=False)]
    for d in range(1, blk):
        send = lax.dynamic_index_in_dim(s, (me + d) % blk, axis=0, keepdims=False)
        pieces.append(lax.ppermute(send, "blk", [(i, (i + d) % blk) for i in range(blk)]))
    got = jnp.stack(pieces, axis=0)
    order = (me - jnp.arange(blk)) % blk
    mine = jnp.take(got, order, axis=0)
    mine = jnp.transpose(mine, (1, 2, 0, 3)).reshape(qt_per, wide * blk * rl)
    block_refs = blk * rl
    keep = jnp.repeat(candidates[0] != 0, block_refs)
    return jnp.where(keep[None, :], mine, jnp.float32(0.0))


def solution(mesh):
    placed = (
        P(("wide", "blk"), None, None),
        P(("wide", "blk"), None, None),
        P(),
        P(),
        P(),
        P(("wide", "blk"), None),
    )
    return jax.shard_map(
        shards, mesh=mesh, in_specs=placed, out_specs=P(("wide", "blk"), None), check_vma=False
    )
```

```python
import math

import jax
import jax.numpy as jnp
from jax import lax
from jax.experimental import pallas as pl
from jax.experimental.pallas import tpu as pltpu
from jax.sharding import PartitionSpec as P

SIDE = 8


epsilon = 1e-06


def conv_table(weights, width):
    count = width * width
    position = jnp.arange(count, dtype=jnp.int32)
    grid_row = position // width
    grid_col = position % width
    delta_row = grid_row[None, :] - grid_row[:, None]
    delta_col = grid_col[None, :] - grid_col[:, None]
    inside = (jnp.abs(delta_row) <= 1) & (jnp.abs(delta_col) <= 1)
    tap_index = (delta_row + 1) * 3 + (delta_col + 1)
    selector = (tap_index[None] == jnp.arange(9, dtype=jnp.int32)[:, None, None]) & inside[None]
    table = jnp.sum(
        jnp.where(selector[None], weights.astype(jnp.float32)[:, :, None, None], jnp.float32(0.0)),
        axis=1,
    )
    return table.astype(jnp.bfloat16)


def normalize(features):
    values = features.astype(jnp.float32)
    inverse_rms = lax.rsqrt(jnp.mean(values * values, axis=-1, keepdims=True) + epsilon)
    return (values * inverse_rms).astype(jnp.bfloat16)


CH = 256


def filter_kernel(q_ref, r_ref, qt_ref, bias_ref, rtt_ref, col_ref, row_ref, c_scr, h_scr, rt_ref, f_scr):
    rows = q_ref.shape[0]
    lanes = r_ref.shape[0]
    chunks = lanes // CH
    hid = rt_ref.shape[0]
    cells = qt_ref.shape[1]
    depth = q_ref.shape[1]
    scale = math.sqrt(depth)

    @pl.when(pl.program_id(0) == 0)
    def _():
        rt_ref[...] = jnp.zeros(rt_ref.shape, rt_ref.dtype)
        for k in range(hid):
            blockk = rtt_ref[k]
            for x in range(CH // cells):
                rt_ref[k, x * cells:(x + 1) * cells, x * cells:(x + 1) * cells] = blockk
    qt = q_ref[...]
    for rc in range(chunks):
        corr = lax.dot_general(
            qt, r_ref[rc * CH:(rc + 1) * CH, :], (((1,), (1,)), ((), ())),
            preferred_element_type=jnp.float32,
        )
        c_scr[:, rc * CH:(rc + 1) * CH] = (corr / scale).astype(jnp.bfloat16)

    nq = rows // cells
    per = hid // 4
    for p in range(nq):
        for rc in range(chunks):
            cc = c_scr[p * cells:(p + 1) * cells, rc * CH:(rc + 1) * CH]
            for kg in range(hid // per):
                hq = jnp.dot(
                    qt_ref[kg * per * cells:(kg + 1) * per * cells, :], cc,
                    preferred_element_type=jnp.float32,
                )
                hq = jnp.maximum(hq + bias_ref[kg * per * cells:(kg + 1) * per * cells, :], 0.0)
                hq = hq.astype(jnp.bfloat16)
                for kk in range(per):
                    k = kg * per + kk
                    row0 = (p * chunks + rc) * cells
                    h_scr[k, row0:row0 + cells, :] = hq[kk * cells:(kk + 1) * cells, :]
    f_scr[...] = jnp.dot(h_scr[0], rt_ref[0], preferred_element_type=jnp.float32)
    for k in range(1, hid):
        f_scr[...] += jnp.dot(h_scr[k], rt_ref[k], preferred_element_type=jnp.float32)
    for p in range(nq):
        acc = f_scr[p * chunks * cells:(p + 1) * chunks * cells, :]
        col_ref[0, p] = jnp.max(acc.reshape(chunks, cells, CH), axis=1)
        accT = acc.T
        row_ref[0, p] = jnp.max(accT.reshape(CH // cells, cells, chunks * cells), axis=1)


def local_scores(q_all, r_all, query_table, ref_table, tap_bias):
    nql, cells, depth = q_all.shape
    nrl = r_all.shape[0]
    hid = query_table.shape[0]
    qt_per = 4
    tiles = nql // qt_per
    chunks = nrl * cells // CH
    r4 = CH // cells
    qstack = query_table.reshape(hid * cells, cells)
    bias_col = jnp.repeat(tap_bias.astype(jnp.float32), cells)[:, None]
    rtT = jnp.transpose(ref_table, (0, 2, 1))
    q2 = q_all.reshape(nql * cells, depth)
    r2 = r_all.reshape(nrl * cells, depth)
    col, row = pl.pallas_call(
        filter_kernel,
        grid=(tiles,),
        in_specs=[
            pl.BlockSpec((qt_per * cells, depth), lambda t: (t, 0)),
            pl.BlockSpec((nrl * cells, depth), lambda t: (0, 0)),
            pl.BlockSpec((hid * cells, cells), lambda t: (0, 0)),
            pl.BlockSpec((hid * cells, 1), lambda t: (0, 0)),
            pl.BlockSpec((hid, cells, cells), lambda t: (0, 0, 0)),
        ],
        out_specs=[
            pl.BlockSpec((1, qt_per, chunks, CH), lambda t: (t, 0, 0, 0)),
            pl.BlockSpec((1, qt_per, r4, chunks * cells), lambda t: (t, 0, 0, 0)),
        ],
        out_shape=[
            jax.ShapeDtypeStruct((tiles, qt_per, chunks, CH), jnp.float32),
            jax.ShapeDtypeStruct((tiles, qt_per, r4, chunks * cells), jnp.float32),
        ],
        scratch_shapes=[
            pltpu.VMEM((qt_per * cells, nrl * cells), jnp.bfloat16),
            pltpu.VMEM((hid, qt_per * chunks * cells, CH), jnp.bfloat16),
            pltpu.VMEM((hid, CH, CH), jnp.bfloat16),
            pltpu.VMEM((qt_per * chunks * cells, CH), jnp.float32),
        ],
        compiler_params=pltpu.CompilerParams(vmem_limit_bytes=56 * 1024 * 1024),
    )(q2, r2, qstack, bias_col, rtT)
    col_pool = jnp.mean(col.reshape(tiles, qt_per, chunks, r4, cells), axis=-1)
    row_pool = jnp.mean(row.reshape(tiles, qt_per, r4, chunks, cells), axis=-1)
    row_pool = jnp.transpose(row_pool, (0, 1, 3, 2))
    return (0.5 * (row_pool + col_pool)).reshape(nql, nrl)


def shards(queries, references, query_taps, ref_taps, tap_bias, candidates):
    query_table = conv_table(query_taps, SIDE)
    ref_table = conv_table(ref_taps, SIDE)
    query_unit = normalize(queries)
    ref_unit = normalize(references)
    blk = lax.axis_size("blk")
    wide = lax.axis_size("wide")
    qt_per = query_unit.shape[0]
    rl = ref_unit.shape[0]
    shifts = [query_unit] + [
        lax.ppermute(query_unit, "blk", [(i, (i + d) % blk) for i in range(blk)])
        for d in range(1, blk)
    ]
    q_all = jnp.concatenate(shifts, axis=0)
    parts = []
    for slot in range(rl):
        r_slot = lax.all_gather(ref_unit[slot:slot + 1], "wide", axis=0, tiled=True)
        parts.append(local_scores(q_all, r_slot, query_table, ref_table, tap_bias))
    s = jnp.stack(parts, axis=-1).reshape(blk, qt_per, wide, rl)
    me = lax.axis_index("blk")
    pieces = [s[0]] + [
        lax.ppermute(s[d], "blk", [(i, (i - d) % blk) for i in range(blk)])
        for d in range(1, blk)
    ]
    got = jnp.stack(pieces, axis=0)
    order = (jnp.arange(blk) - me) % blk
    mine = jnp.take(got, order, axis=0)
    mine = jnp.transpose(mine, (1, 2, 0, 3)).reshape(qt_per, wide * blk * rl)
    block_refs = blk * rl
    keep = jnp.repeat(candidates[0] != 0, block_refs)
    return jnp.where(keep[None, :], mine, jnp.float32(0.0))


def solution(mesh):
    placed = (
        P(("wide", "blk"), None, None),
        P(("wide", "blk"), None, None),
        P(),
        P(),
        P(),
        P(("wide", "blk"), None),
    )
    return jax.shard_map(
        shards, mesh=mesh, in_specs=placed, out_specs=P(("wide", "blk"), None), check_vma=False
    )
```

```python
import math

import jax
import jax.numpy as jnp
from jax import lax
from jax.experimental import pallas as pl
from jax.experimental.pallas import tpu as pltpu
from jax.sharding import PartitionSpec as P

SIDE = 8


epsilon = 1e-06


def conv_table(weights, width):
    count = width * width
    position = jnp.arange(count, dtype=jnp.int32)
    grid_row = position // width
    grid_col = position % width
    delta_row = grid_row[None, :] - grid_row[:, None]
    delta_col = grid_col[None, :] - grid_col[:, None]
    inside = (jnp.abs(delta_row) <= 1) & (jnp.abs(delta_col) <= 1)
    tap_index = (delta_row + 1) * 3 + (delta_col + 1)
    selector = (tap_index[None] == jnp.arange(9, dtype=jnp.int32)[:, None, None]) & inside[None]
    table = jnp.sum(
        jnp.where(selector[None], weights.astype(jnp.float32)[:, :, None, None], jnp.float32(0.0)),
        axis=1,
    )
    return table.astype(jnp.bfloat16)


def normalize(features):
    values = features.astype(jnp.float32)
    inverse_rms = lax.rsqrt(jnp.mean(values * values, axis=-1, keepdims=True) + epsilon)
    return (values * inverse_rms).astype(jnp.bfloat16)


CH = 256


def filter_kernel(q_ref, r_ref, qt_ref, bias_ref, rtt_ref, col_ref, row_ref, c_scr, h_scr, rt_ref, f_scr):
    rows = q_ref.shape[0]
    lanes = r_ref.shape[0]
    chunks = lanes // CH
    hid = rt_ref.shape[0]
    cells = qt_ref.shape[1]
    depth = q_ref.shape[1]
    scale = math.sqrt(depth)

    @pl.when(pl.program_id(0) == 0)
    def _():
        rt_ref[...] = jnp.zeros(rt_ref.shape, rt_ref.dtype)
        for k in range(hid):
            blockk = rtt_ref[k]
            for x in range(CH // cells):
                rt_ref[k, x * cells:(x + 1) * cells, x * cells:(x + 1) * cells] = blockk
    qt = q_ref[...]
    for rc in range(chunks):
        corr = lax.dot_general(
            qt, r_ref[rc * CH:(rc + 1) * CH, :], (((1,), (1,)), ((), ())),
            preferred_element_type=jnp.float32,
        )
        c_scr[:, rc * CH:(rc + 1) * CH] = (corr / scale).astype(jnp.bfloat16)

    nq = rows // cells
    per = hid // 4
    for p in range(nq):
        for rc in range(chunks):
            cc = c_scr[p * cells:(p + 1) * cells, rc * CH:(rc + 1) * CH]
            for kg in range(hid // per):
                hq = jnp.dot(
                    qt_ref[kg * per * cells:(kg + 1) * per * cells, :], cc,
                    preferred_element_type=jnp.float32,
                )
                hq = jnp.maximum(hq + bias_ref[kg * per * cells:(kg + 1) * per * cells, :], 0.0)
                hq = hq.astype(jnp.bfloat16)
                for kk in range(per):
                    k = kg * per + kk
                    row0 = (p * chunks + rc) * cells
                    h_scr[k, row0:row0 + cells, :] = hq[kk * cells:(kk + 1) * cells, :]
    f_scr[...] = jnp.dot(h_scr[0], rt_ref[0], preferred_element_type=jnp.float32)
    for k in range(1, hid):
        f_scr[...] += jnp.dot(h_scr[k], rt_ref[k], preferred_element_type=jnp.float32)
    for p in range(nq):
        acc = f_scr[p * chunks * cells:(p + 1) * chunks * cells, :]
        col_ref[0, p] = jnp.max(acc.reshape(chunks, cells, CH), axis=1)
        accT = acc.T
        row_ref[0, p] = jnp.max(accT.reshape(CH // cells, cells, chunks * cells), axis=1)


def local_scores(q_all, r_all, query_table, ref_table, tap_bias):
    nql, cells, depth = q_all.shape
    nrl = r_all.shape[0]
    hid = query_table.shape[0]
    qt_per = 4
    tiles = nql // qt_per
    chunks = nrl * cells // CH
    r4 = CH // cells
    qstack = query_table.reshape(hid * cells, cells)
    bias_col = jnp.repeat(tap_bias.astype(jnp.float32), cells)[:, None]
    rtT = jnp.transpose(ref_table, (0, 2, 1))
    q2 = q_all.reshape(nql * cells, depth)
    r2 = r_all.reshape(nrl * cells, depth)
    col, row = pl.pallas_call(
        filter_kernel,
        grid=(tiles,),
        in_specs=[
            pl.BlockSpec((qt_per * cells, depth), lambda t: (t, 0)),
            pl.BlockSpec((nrl * cells, depth), lambda t: (0, 0)),
            pl.BlockSpec((hid * cells, cells), lambda t: (0, 0)),
            pl.BlockSpec((hid * cells, 1), lambda t: (0, 0)),
            pl.BlockSpec((hid, cells, cells), lambda t: (0, 0, 0)),
        ],
        out_specs=[
            pl.BlockSpec((1, qt_per, chunks, CH), lambda t: (t, 0, 0, 0)),
            pl.BlockSpec((1, qt_per, r4, chunks * cells), lambda t: (t, 0, 0, 0)),
        ],
        out_shape=[
            jax.ShapeDtypeStruct((tiles, qt_per, chunks, CH), jnp.float32),
            jax.ShapeDtypeStruct((tiles, qt_per, r4, chunks * cells), jnp.float32),
        ],
        scratch_shapes=[
            pltpu.VMEM((qt_per * cells, nrl * cells), jnp.bfloat16),
            pltpu.VMEM((hid, qt_per * chunks * cells, CH), jnp.bfloat16),
            pltpu.VMEM((hid, CH, CH), jnp.bfloat16),
            pltpu.VMEM((qt_per * chunks * cells, CH), jnp.float32),
        ],
        compiler_params=pltpu.CompilerParams(vmem_limit_bytes=56 * 1024 * 1024),
    )(q2, r2, qstack, bias_col, rtT)
    col_pool = jnp.mean(col.reshape(tiles, qt_per, chunks, r4, cells), axis=-1)
    row_pool = jnp.mean(row.reshape(tiles, qt_per, r4, chunks, cells), axis=-1)
    row_pool = jnp.transpose(row_pool, (0, 1, 3, 2))
    return (0.5 * (row_pool + col_pool)).reshape(nql, nrl)


def shards(queries, references, query_taps, ref_taps, tap_bias, candidates):
    query_table = conv_table(query_taps, SIDE)
    ref_table = conv_table(ref_taps, SIDE)
    query_unit = normalize(queries)
    ref_unit = normalize(references)
    blk = lax.axis_size("blk")
    wide = lax.axis_size("wide")
    qt_per = query_unit.shape[0]
    rl = ref_unit.shape[0]
    me = lax.axis_index("blk")
    me_w = lax.axis_index("wide")
    q_all = lax.all_gather(query_unit, "blk", axis=0, tiled=True)
    r0 = jnp.concatenate([ref_unit[0:1]] + [
        lax.ppermute(ref_unit[0:1], "wide", [(i, (i + d) % wide) for i in range(wide)])
        for d in range(1, wide)
    ], axis=0)
    s0 = local_scores(q_all, r0, query_table, ref_table, tap_bias)
    s0 = jnp.take(s0, (me_w - jnp.arange(wide)) % wide, axis=1)
    r1 = lax.all_gather(ref_unit[1:2], "wide", axis=0, tiled=True)
    s1 = local_scores(q_all, r1, query_table, ref_table, tap_bias)

    def scatter(part):
        part = part.reshape(blk, qt_per, wide)
        pieces = [lax.dynamic_index_in_dim(part, me, axis=0, keepdims=False)]
        for d in range(1, blk):
            send = lax.dynamic_index_in_dim(part, (me + d) % blk, axis=0, keepdims=False)
            pieces.append(lax.ppermute(send, "blk", [(i, (i + d) % blk) for i in range(blk)]))
        got = jnp.stack(pieces, axis=0)
        return jnp.take(got, (me - jnp.arange(blk)) % blk, axis=0)

    mine = jnp.stack([scatter(s0), scatter(s1)], axis=-1)
    mine = jnp.transpose(mine, (1, 2, 0, 3)).reshape(qt_per, wide * blk * rl)
    block_refs = blk * rl
    keep = jnp.repeat(candidates[0] != 0, block_refs)
    return jnp.where(keep[None, :], mine, jnp.float32(0.0))


def solution(mesh):
    placed = (
        P(("wide", "blk"), None, None),
        P(("wide", "blk"), None, None),
        P(),
        P(),
        P(),
        P(("wide", "blk"), None),
    )
    return jax.shard_map(
        shards, mesh=mesh, in_specs=placed, out_specs=P(("wide", "blk"), None), check_vma=False
    )
```

```python
import math

import jax
import jax.numpy as jnp
from jax import lax
from jax.experimental import pallas as pl
from jax.experimental.pallas import tpu as pltpu
from jax.sharding import PartitionSpec as P

SIDE = 8


epsilon = 1e-06


def conv_table(weights, width):
    count = width * width
    position = jnp.arange(count, dtype=jnp.int32)
    grid_row = position // width
    grid_col = position % width
    delta_row = grid_row[None, :] - grid_row[:, None]
    delta_col = grid_col[None, :] - grid_col[:, None]
    inside = (jnp.abs(delta_row) <= 1) & (jnp.abs(delta_col) <= 1)
    tap_index = (delta_row + 1) * 3 + (delta_col + 1)
    selector = (tap_index[None] == jnp.arange(9, dtype=jnp.int32)[:, None, None]) & inside[None]
    table = jnp.sum(
        jnp.where(selector[None], weights.astype(jnp.float32)[:, :, None, None], jnp.float32(0.0)),
        axis=1,
    )
    return table.astype(jnp.bfloat16)


def normalize(features):
    values = features.astype(jnp.float32)
    inverse_rms = lax.rsqrt(jnp.mean(values * values, axis=-1, keepdims=True) + epsilon)
    return (values * inverse_rms).astype(jnp.bfloat16)


CH = 256


def filter_kernel(q_ref, r_ref, qt_ref, bias_ref, rtt_ref, col_ref, row_ref, c_scr, h_scr, rt_ref, f_scr):
    rows = q_ref.shape[0]
    lanes = r_ref.shape[0]
    chunks = lanes // CH
    hid = rt_ref.shape[0]
    cells = qt_ref.shape[1]
    depth = q_ref.shape[1]
    scale = math.sqrt(depth)

    @pl.when(pl.program_id(0) == 0)
    def _():
        rt_ref[...] = jnp.zeros(rt_ref.shape, rt_ref.dtype)
        for k in range(hid):
            blockk = rtt_ref[k]
            for x in range(CH // cells):
                rt_ref[k, x * cells:(x + 1) * cells, x * cells:(x + 1) * cells] = blockk
    qt = q_ref[...]
    for rc in range(chunks):
        corr = lax.dot_general(
            qt, r_ref[rc * CH:(rc + 1) * CH, :], (((1,), (1,)), ((), ())),
            preferred_element_type=jnp.float32,
        )
        c_scr[:, rc * CH:(rc + 1) * CH] = (corr / scale).astype(jnp.bfloat16)

    nq = rows // cells
    per = hid // 4
    for p in range(nq):
        for rc in range(chunks):
            cc = c_scr[p * cells:(p + 1) * cells, rc * CH:(rc + 1) * CH]
            for kg in range(hid // per):
                hq = jnp.dot(
                    qt_ref[kg * per * cells:(kg + 1) * per * cells, :], cc,
                    preferred_element_type=jnp.float32,
                )
                hq = jnp.maximum(hq + bias_ref[kg * per * cells:(kg + 1) * per * cells, :], 0.0)
                hq = hq.astype(jnp.bfloat16)
                for kk in range(per):
                    k = kg * per + kk
                    row0 = (p * chunks + rc) * cells
                    h_scr[k, row0:row0 + cells, :] = hq[kk * cells:(kk + 1) * cells, :]
    f_scr[...] = jnp.dot(h_scr[0], rt_ref[0], preferred_element_type=jnp.float32)
    for k in range(1, hid):
        f_scr[...] += jnp.dot(h_scr[k], rt_ref[k], preferred_element_type=jnp.float32)
    for p in range(nq):
        acc = f_scr[p * chunks * cells:(p + 1) * chunks * cells, :]
        col_ref[0, p] = jnp.max(acc.reshape(chunks, cells, CH), axis=1)
        accT = acc.T
        row_ref[0, p] = jnp.max(accT.reshape(CH // cells, cells, chunks * cells), axis=1)


def local_scores(q_all, r_all, query_table, ref_table, tap_bias):
    nql, cells, depth = q_all.shape
    nrl = r_all.shape[0]
    hid = query_table.shape[0]
    qt_per = 4
    tiles = nql // qt_per
    chunks = nrl * cells // CH
    r4 = CH // cells
    qstack = query_table.reshape(hid * cells, cells)
    bias_col = jnp.repeat(tap_bias.astype(jnp.float32), cells)[:, None]
    rtT = jnp.transpose(ref_table, (0, 2, 1))
    q2 = q_all.reshape(nql * cells, depth)
    r2 = r_all.reshape(nrl * cells, depth)
    col, row = pl.pallas_call(
        filter_kernel,
        grid=(tiles,),
        in_specs=[
            pl.BlockSpec((qt_per * cells, depth), lambda t: (t, 0)),
            pl.BlockSpec((nrl * cells, depth), lambda t: (0, 0)),
            pl.BlockSpec((hid * cells, cells), lambda t: (0, 0)),
            pl.BlockSpec((hid * cells, 1), lambda t: (0, 0)),
            pl.BlockSpec((hid, cells, cells), lambda t: (0, 0, 0)),
        ],
        out_specs=[
            pl.BlockSpec((1, qt_per, chunks, CH), lambda t: (t, 0, 0, 0)),
            pl.BlockSpec((1, qt_per, r4, chunks * cells), lambda t: (t, 0, 0, 0)),
        ],
        out_shape=[
            jax.ShapeDtypeStruct((tiles, qt_per, chunks, CH), jnp.float32),
            jax.ShapeDtypeStruct((tiles, qt_per, r4, chunks * cells), jnp.float32),
        ],
        scratch_shapes=[
            pltpu.VMEM((qt_per * cells, nrl * cells), jnp.bfloat16),
            pltpu.VMEM((hid, qt_per * chunks * cells, CH), jnp.bfloat16),
            pltpu.VMEM((hid, CH, CH), jnp.bfloat16),
            pltpu.VMEM((qt_per * chunks * cells, CH), jnp.float32),
        ],
        compiler_params=pltpu.CompilerParams(vmem_limit_bytes=56 * 1024 * 1024),
    )(q2, r2, qstack, bias_col, rtT)
    col_pool = jnp.mean(col.reshape(tiles, qt_per, chunks, r4, cells), axis=-1)
    row_pool = jnp.mean(row.reshape(tiles, qt_per, r4, chunks, cells), axis=-1)
    row_pool = jnp.transpose(row_pool, (0, 1, 3, 2))
    return (0.5 * (row_pool + col_pool)).reshape(nql, nrl)


def shards(queries, references, query_taps, ref_taps, tap_bias, candidates):
    query_table = conv_table(query_taps, SIDE)
    ref_table = conv_table(ref_taps, SIDE)
    query_unit = normalize(queries)
    ref_unit = normalize(references)
    blk = lax.axis_size("blk")
    wide = lax.axis_size("wide")
    qt_per = query_unit.shape[0]
    rl = ref_unit.shape[0]
    shifts = [query_unit] + [
        lax.ppermute(query_unit, "blk", [(i, (i + d) % blk) for i in range(blk)])
        for d in range(1, blk)
    ]
    q_all = jnp.concatenate(shifts, axis=0)
    parts = []
    for slot in range(rl):
        r_slot = lax.all_gather(ref_unit[slot:slot + 1], "wide", axis=0, tiled=True)
        parts.append(local_scores(q_all, r_slot, query_table, ref_table, tap_bias))
    s = jnp.stack(parts, axis=-1).reshape(blk, qt_per, wide, rl)
    me = lax.axis_index("blk")
    outgoing = jnp.take(s, (me - jnp.arange(blk)) % blk, axis=0)
    mine = lax.all_to_all(outgoing, "blk", 0, 0, tiled=True)
    mine = jnp.transpose(mine, (1, 2, 0, 3)).reshape(qt_per, wide * blk * rl)
    block_refs = blk * rl
    keep = jnp.repeat(candidates[0] != 0, block_refs)
    return jnp.where(keep[None, :], mine, jnp.float32(0.0))


def solution(mesh):
    placed = (
        P(("wide", "blk"), None, None),
        P(("wide", "blk"), None, None),
        P(),
        P(),
        P(),
        P(("wide", "blk"), None),
    )
    return jax.shard_map(
        shards, mesh=mesh, in_specs=placed, out_specs=P(("wide", "blk"), None), check_vma=False
    )
```

```python
import math

import jax
import jax.numpy as jnp
from jax import lax
from jax.experimental import pallas as pl
from jax.experimental.pallas import tpu as pltpu
from jax.sharding import PartitionSpec as P

SIDE = 8


epsilon = 1e-06


def conv_table(weights, width):
    count = width * width
    position = jnp.arange(count, dtype=jnp.int32)
    grid_row = position // width
    grid_col = position % width
    delta_row = grid_row[None, :] - grid_row[:, None]
    delta_col = grid_col[None, :] - grid_col[:, None]
    inside = (jnp.abs(delta_row) <= 1) & (jnp.abs(delta_col) <= 1)
    tap_index = (delta_row + 1) * 3 + (delta_col + 1)
    selector = (tap_index[None] == jnp.arange(9, dtype=jnp.int32)[:, None, None]) & inside[None]
    table = jnp.sum(
        jnp.where(selector[None], weights.astype(jnp.float32)[:, :, None, None], jnp.float32(0.0)),
        axis=1,
    )
    return table.astype(jnp.bfloat16)


def normalize(features):
    values = features.astype(jnp.float32)
    inverse_rms = lax.rsqrt(jnp.mean(values * values, axis=-1, keepdims=True) + epsilon)
    return (values * inverse_rms).astype(jnp.bfloat16)


CH = 256


GB = 4


def filter_kernel(idx_ref, cnt_ref, q_ref, r_ref, qt_ref, bias_ref, rtt_ref, col_ref, row_ref,
                  c_scr, h_scr, rt_ref, f_scr):
    t = pl.program_id(0)
    rows = q_ref.shape[0]
    hid = rtt_ref.shape[0]
    cells = rtt_ref.shape[1]
    depth = q_ref.shape[1]
    nq = rows // cells
    r4 = CH // cells
    br = r4 // 2
    groups = col_ref.shape[2] // 2
    scale = math.sqrt(depth)
    per = hid // 4

    @pl.when(t == 0)
    def _():
        rt_ref[...] = jnp.zeros(rt_ref.shape, rt_ref.dtype)
        for k in range(hid):
            blockk = rtt_ref[k]
            for x in range(r4):
                rt_ref[k, x * cells:(x + 1) * cells, x * cells:(x + 1) * cells] = blockk

    qt = q_ref[...]
    for g in range(groups):
        @pl.when(g * GB < cnt_ref[t])
        def _():
            for slot in range(GB):
                blk_id = idx_ref[t, g * GB + slot]
                start = pl.multiple_of(blk_id * (br * cells), br * cells)
                corr = lax.dot_general(
                    qt, r_ref[pl.ds(start, br * cells), :], (((1,), (1,)), ((), ())),
                    preferred_element_type=jnp.float32,
                )
                c_scr[:, slot * br * cells:(slot + 1) * br * cells] = (corr / scale).astype(jnp.bfloat16)
            for p in range(nq):
                for c2 in range(2):
                    cc = c_scr[p * cells:(p + 1) * cells, c2 * CH:(c2 + 1) * CH]
                    for kg in range(hid // per):
                        hq = jnp.dot(
                            qt_ref[kg * per * cells:(kg + 1) * per * cells, :], cc,
                            preferred_element_type=jnp.float32,
                        )
                        hq = jnp.maximum(hq + bias_ref[kg * per * cells:(kg + 1) * per * cells, :], 0.0)
                        hq = hq.astype(jnp.bfloat16)
                        for kk in range(per):
                            k = kg * per + kk
                            row0 = (p * 2 + c2) * cells
                            h_scr[k, row0:row0 + cells, :] = hq[kk * cells:(kk + 1) * cells, :]
            f_scr[...] = jnp.dot(h_scr[0], rt_ref[0], preferred_element_type=jnp.float32)
            for k in range(1, hid):
                f_scr[...] += jnp.dot(h_scr[k], rt_ref[k], preferred_element_type=jnp.float32)
            for p in range(nq):
                acc = f_scr[p * 2 * cells:(p + 1) * 2 * cells, :]
                col_ref[0, p, 2 * g:2 * g + 2, :] = jnp.max(acc.reshape(2, cells, CH), axis=1)
                accT = acc.T
                row_ref[0, p, :, 2 * g * cells:(2 * g + 2) * cells] = jnp.max(
                    accT.reshape(r4, cells, 2 * cells), axis=1)


def local_scores(q_all, r_all, cand, query_table, ref_table, tap_bias):
    nql, cells, depth = q_all.shape
    nrl = r_all.shape[0]
    hid = query_table.shape[0]
    qt_per = 4
    tiles = nql // qt_per
    nb = cand.shape[1]
    br = nrl // nb
    chunks = nrl * cells // CH
    r4 = CH // cells
    keep = (cand != 0).astype(jnp.int32)
    idx = jnp.argsort(1 - keep, axis=1, stable=True).astype(jnp.int32)
    cnt = jnp.sum(keep, axis=1).astype(jnp.int32)
    qstack = query_table.reshape(hid * cells, cells)
    bias_col = jnp.repeat(tap_bias.astype(jnp.float32), cells)[:, None]
    rtT = jnp.transpose(ref_table, (0, 2, 1))
    q2 = q_all.reshape(nql * cells, depth)
    r2 = r_all.reshape(nrl * cells, depth)
    col, row = pl.pallas_call(
        filter_kernel,
        grid_spec=pltpu.PrefetchScalarGridSpec(
            num_scalar_prefetch=2,
            grid=(tiles,),
            in_specs=[
                pl.BlockSpec((qt_per * cells, depth), lambda t, i, c: (t, 0)),
                pl.BlockSpec((nrl * cells, depth), lambda t, i, c: (0, 0)),
                pl.BlockSpec((hid * cells, cells), lambda t, i, c: (0, 0)),
                pl.BlockSpec((hid * cells, 1), lambda t, i, c: (0, 0)),
                pl.BlockSpec((hid, cells, cells), lambda t, i, c: (0, 0, 0)),
            ],
            out_specs=[
                pl.BlockSpec((1, qt_per, chunks, CH), lambda t, i, c: (t, 0, 0, 0)),
                pl.BlockSpec((1, qt_per, r4, chunks * cells), lambda t, i, c: (t, 0, 0, 0)),
            ],
            scratch_shapes=[
                pltpu.VMEM((qt_per * cells, GB * br * cells), jnp.bfloat16),
                pltpu.VMEM((hid, qt_per * 2 * cells, CH), jnp.bfloat16),
                pltpu.VMEM((hid, CH, CH), jnp.bfloat16),
                pltpu.VMEM((qt_per * 2 * cells, CH), jnp.float32),
            ],
        ),
        out_shape=[
            jax.ShapeDtypeStruct((tiles, qt_per, chunks, CH), jnp.float32),
            jax.ShapeDtypeStruct((tiles, qt_per, r4, chunks * cells), jnp.float32),
        ],
        compiler_params=pltpu.CompilerParams(vmem_limit_bytes=56 * 1024 * 1024),
    )(idx, cnt, q2, r2, qstack, bias_col, rtT)
    col_pool = jnp.mean(col.reshape(tiles, qt_per, chunks, r4, cells), axis=-1)
    row_pool = jnp.mean(row.reshape(tiles, qt_per, r4, chunks, cells), axis=-1)
    row_pool = jnp.transpose(row_pool, (0, 1, 3, 2))
    packed = (0.5 * (row_pool + col_pool)).reshape(tiles, qt_per, nb, br)
    where_is = jnp.argsort(idx, axis=1)
    return jnp.take_along_axis(packed, where_is[:, None, :, None], axis=2)


def shards(queries, references, query_taps, ref_taps, tap_bias, candidates):
    query_table = conv_table(query_taps, SIDE)
    ref_table = conv_table(ref_taps, SIDE)
    query_unit = normalize(queries)
    ref_unit = normalize(references)
    blk = lax.axis_size("blk")
    wide = lax.axis_size("wide")
    qt_per = query_unit.shape[0]
    rl = ref_unit.shape[0]
    me = lax.axis_index("blk")
    payload = jnp.concatenate(
        [query_unit.reshape(-1), candidates.reshape(-1).astype(jnp.bfloat16)])
    pieces = [payload] + [
        lax.ppermute(payload, "blk", [(i, (i + d) % blk) for i in range(blk)])
        for d in range(1, blk)
    ]
    qsize = query_unit.size
    q_all = jnp.concatenate([x[:qsize] for x in pieces]).reshape(
        (blk * qt_per,) + query_unit.shape[1:])
    cand = jnp.stack([x[qsize:] for x in pieces])
    r_all = lax.all_gather(ref_unit, "wide", axis=0, tiled=True)
    s = local_scores(q_all, r_all, cand, query_table, ref_table, tap_bias)
    outgoing = jnp.take(s, (me - jnp.arange(blk)) % blk, axis=0)
    mine = lax.all_to_all(outgoing, "blk", 0, 0, tiled=True)
    mine = jnp.transpose(mine, (1, 2, 0, 3)).reshape(qt_per, wide * blk * rl)
    block_refs = blk * rl
    keep = jnp.repeat(candidates[0] != 0, block_refs)
    return jnp.where(keep[None, :], mine, jnp.float32(0.0))


def solution(mesh):
    placed = (
        P(("wide", "blk"), None, None),
        P(("wide", "blk"), None, None),
        P(),
        P(),
        P(),
        P(("wide", "blk"), None),
    )
    return jax.shard_map(
        shards, mesh=mesh, in_specs=placed, out_specs=P(("wide", "blk"), None), check_vma=False
    )
```

```python
import math

import jax
import jax.numpy as jnp
from jax import lax
from jax.experimental import pallas as pl
from jax.experimental.pallas import tpu as pltpu
from jax.sharding import PartitionSpec as P

SIDE = 8


epsilon = 1e-06


def conv_table(weights, width):
    count = width * width
    position = jnp.arange(count, dtype=jnp.int32)
    grid_row = position // width
    grid_col = position % width
    delta_row = grid_row[None, :] - grid_row[:, None]
    delta_col = grid_col[None, :] - grid_col[:, None]
    inside = (jnp.abs(delta_row) <= 1) & (jnp.abs(delta_col) <= 1)
    tap_index = (delta_row + 1) * 3 + (delta_col + 1)
    selector = (tap_index[None] == jnp.arange(9, dtype=jnp.int32)[:, None, None]) & inside[None]
    table = jnp.sum(
        jnp.where(selector[None], weights.astype(jnp.float32)[:, :, None, None], jnp.float32(0.0)),
        axis=1,
    )
    return table.astype(jnp.bfloat16)


def normalize(features):
    values = features.astype(jnp.float32)
    inverse_rms = lax.rsqrt(jnp.mean(values * values, axis=-1, keepdims=True) + epsilon)
    return (values * inverse_rms).astype(jnp.bfloat16)


CH = 256


GB = 4


def filter_kernel(idx_ref, cnt_ref, q_ref, r_ref, qt_ref, bias_ref, rtt_ref, col_ref, row_ref,
                  c_scr, h_scr, rt_ref, f_scr):
    t = pl.program_id(0)
    rows = q_ref.shape[0]
    hid = rtt_ref.shape[0]
    cells = rtt_ref.shape[1]
    depth = q_ref.shape[1]
    nq = rows // cells
    r4 = CH // cells
    br = r4 // 2
    groups = col_ref.shape[2] // 2
    scale = math.sqrt(depth)
    per = hid // 4

    @pl.when(t == 0)
    def _():
        rt_ref[...] = jnp.zeros(rt_ref.shape, rt_ref.dtype)
        for k in range(hid):
            blockk = rtt_ref[k]
            for x in range(r4):
                rt_ref[k, x * cells:(x + 1) * cells, x * cells:(x + 1) * cells] = blockk

    qt = q_ref[...]
    for g in range(groups):
        @pl.when(g * GB < cnt_ref[t])
        def _():
            for slot in range(GB):
                blk_id = idx_ref[t, g * GB + slot]
                start = pl.multiple_of(blk_id * (br * cells), br * cells)
                corr = lax.dot_general(
                    qt, r_ref[pl.ds(start, br * cells), :], (((1,), (1,)), ((), ())),
                    preferred_element_type=jnp.float32,
                )
                c_scr[:, slot * br * cells:(slot + 1) * br * cells] = (corr / scale).astype(jnp.bfloat16)
            for p in range(nq):
                for c2 in range(2):
                    cc = c_scr[p * cells:(p + 1) * cells, c2 * CH:(c2 + 1) * CH]
                    for kg in range(hid // per):
                        hq = jnp.dot(
                            qt_ref[kg * per * cells:(kg + 1) * per * cells, :], cc,
                            preferred_element_type=jnp.float32,
                        )
                        hq = jnp.maximum(hq + bias_ref[kg * per * cells:(kg + 1) * per * cells, :], 0.0)
                        hq = hq.astype(jnp.bfloat16)
                        for kk in range(per):
                            k = kg * per + kk
                            row0 = (p * 2 + c2) * cells
                            h_scr[k, row0:row0 + cells, :] = hq[kk * cells:(kk + 1) * cells, :]
            f_scr[...] = jnp.dot(h_scr[0], rt_ref[0], preferred_element_type=jnp.float32)
            for k in range(1, hid):
                f_scr[...] += jnp.dot(h_scr[k], rt_ref[k], preferred_element_type=jnp.float32)
            for p in range(nq):
                acc = f_scr[p * 2 * cells:(p + 1) * 2 * cells, :]
                col_ref[0, p, 2 * g:2 * g + 2, :] = jnp.max(acc.reshape(2, cells, CH), axis=1)
                accT = acc.T
                row_ref[0, p, :, 2 * g * cells:(2 * g + 2) * cells] = jnp.max(
                    accT.reshape(r4, cells, 2 * cells), axis=1)


def local_scores(q_all, r_all, cand, query_table, ref_table, tap_bias):
    nql, cells, depth = q_all.shape
    nrl = r_all.shape[0]
    hid = query_table.shape[0]
    qt_per = 4
    tiles = nql // qt_per
    nb = cand.shape[1]
    br = nrl // nb
    chunks = nrl * cells // CH
    r4 = CH // cells
    keep = (cand != 0).astype(jnp.int32)
    idx = jnp.argsort(1 - keep, axis=1, stable=True).astype(jnp.int32)
    cnt = jnp.sum(keep, axis=1).astype(jnp.int32)
    qstack = query_table.reshape(hid * cells, cells)
    bias_col = jnp.repeat(tap_bias.astype(jnp.float32), cells)[:, None]
    rtT = jnp.transpose(ref_table, (0, 2, 1))
    q2 = q_all.reshape(nql * cells, depth)
    r2 = r_all.reshape(nrl * cells, depth)
    col, row = pl.pallas_call(
        filter_kernel,
        grid_spec=pltpu.PrefetchScalarGridSpec(
            num_scalar_prefetch=2,
            grid=(tiles,),
            in_specs=[
                pl.BlockSpec((qt_per * cells, depth), lambda t, i, c: (t, 0)),
                pl.BlockSpec((nrl * cells, depth), lambda t, i, c: (0, 0)),
                pl.BlockSpec((hid * cells, cells), lambda t, i, c: (0, 0)),
                pl.BlockSpec((hid * cells, 1), lambda t, i, c: (0, 0)),
                pl.BlockSpec((hid, cells, cells), lambda t, i, c: (0, 0, 0)),
            ],
            out_specs=[
                pl.BlockSpec((1, qt_per, chunks, CH), lambda t, i, c: (t, 0, 0, 0)),
                pl.BlockSpec((1, qt_per, r4, chunks * cells), lambda t, i, c: (t, 0, 0, 0)),
            ],
            scratch_shapes=[
                pltpu.VMEM((qt_per * cells, GB * br * cells), jnp.bfloat16),
                pltpu.VMEM((hid, qt_per * 2 * cells, CH), jnp.bfloat16),
                pltpu.VMEM((hid, CH, CH), jnp.bfloat16),
                pltpu.VMEM((qt_per * 2 * cells, CH), jnp.float32),
            ],
        ),
        out_shape=[
            jax.ShapeDtypeStruct((tiles, qt_per, chunks, CH), jnp.float32),
            jax.ShapeDtypeStruct((tiles, qt_per, r4, chunks * cells), jnp.float32),
        ],
        compiler_params=pltpu.CompilerParams(vmem_limit_bytes=56 * 1024 * 1024),
    )(idx, cnt, q2, r2, qstack, bias_col, rtT)
    col_pool = jnp.mean(col.reshape(tiles, qt_per, chunks, r4, cells), axis=-1)
    row_pool = jnp.mean(row.reshape(tiles, qt_per, r4, chunks, cells), axis=-1)
    row_pool = jnp.transpose(row_pool, (0, 1, 3, 2))
    packed = (0.5 * (row_pool + col_pool)).reshape(tiles, qt_per, nb, br)
    where_is = jnp.argsort(idx, axis=1)
    return jnp.take_along_axis(packed, where_is[:, None, :, None], axis=2)


def shards(queries, references, query_taps, ref_taps, tap_bias, candidates):
    query_table = conv_table(query_taps, SIDE)
    ref_table = conv_table(ref_taps, SIDE)
    ref_unit = normalize(references)
    ref_unit, queries = lax.optimization_barrier((ref_unit, queries))
    r_all = lax.all_gather(ref_unit, "wide", axis=0, tiled=True)
    query_unit = normalize(queries)
    blk = lax.axis_size("blk")
    wide = lax.axis_size("wide")
    qt_per = query_unit.shape[0]
    rl = ref_unit.shape[0]
    me = lax.axis_index("blk")
    payload = jnp.concatenate(
        [query_unit.reshape(-1), candidates.reshape(-1).astype(jnp.bfloat16)])
    pieces = [payload] + [
        lax.ppermute(payload, "blk", [(i, (i + d) % blk) for i in range(blk)])
        for d in range(1, blk)
    ]
    qsize = query_unit.size
    q_all = jnp.concatenate([x[:qsize] for x in pieces]).reshape(
        (blk * qt_per,) + query_unit.shape[1:])
    cand = jnp.stack([x[qsize:] for x in pieces])
    s = local_scores(q_all, r_all, cand, query_table, ref_table, tap_bias)
    outgoing = jnp.take(s, (me - jnp.arange(blk)) % blk, axis=0)
    mine = lax.all_to_all(outgoing, "blk", 0, 0, tiled=True)
    mine = jnp.transpose(mine, (1, 2, 0, 3)).reshape(qt_per, wide * blk * rl)
    block_refs = blk * rl
    keep = jnp.repeat(candidates[0] != 0, block_refs)
    return jnp.where(keep[None, :], mine, jnp.float32(0.0))


def solution(mesh):
    placed = (
        P(("wide", "blk"), None, None),
        P(("wide", "blk"), None, None),
        P(),
        P(),
        P(),
        P(("wide", "blk"), None),
    )
    return jax.shard_map(
        shards, mesh=mesh, in_specs=placed, out_specs=P(("wide", "blk"), None), check_vma=False
    )
```

```python
import math

import jax
import jax.numpy as jnp
from jax import lax
from jax.experimental import pallas as pl
from jax.experimental.pallas import tpu as pltpu
from jax.sharding import PartitionSpec as P

SIDE = 8


epsilon = 1e-06


def conv_table(weights, width):
    count = width * width
    position = jnp.arange(count, dtype=jnp.int32)
    grid_row = position // width
    grid_col = position % width
    delta_row = grid_row[None, :] - grid_row[:, None]
    delta_col = grid_col[None, :] - grid_col[:, None]
    inside = (jnp.abs(delta_row) <= 1) & (jnp.abs(delta_col) <= 1)
    tap_index = (delta_row + 1) * 3 + (delta_col + 1)
    selector = (tap_index[None] == jnp.arange(9, dtype=jnp.int32)[:, None, None]) & inside[None]
    table = jnp.sum(
        jnp.where(selector[None], weights.astype(jnp.float32)[:, :, None, None], jnp.float32(0.0)),
        axis=1,
    )
    return table.astype(jnp.bfloat16)


def normalize(features):
    values = features.astype(jnp.float32)
    inverse_rms = lax.rsqrt(jnp.mean(values * values, axis=-1, keepdims=True) + epsilon)
    return (values * inverse_rms).astype(jnp.bfloat16)


CH = 256


GB = 4


def filter_kernel(idx_ref, cnt_ref, q_ref, r_ref, qt_ref, bias_ref, rtt_ref, col_ref, row_ref,
                  c_scr, h_scr, rt_ref, f_scr):
    t = pl.program_id(0)
    rows = q_ref.shape[0]
    hid = rtt_ref.shape[0]
    cells = rtt_ref.shape[1]
    depth = q_ref.shape[1]
    nq = rows // cells
    r4 = CH // cells
    br = r4 // 2
    groups = col_ref.shape[2] // 2
    scale = math.sqrt(depth)
    per = hid // 4

    @pl.when(t == 0)
    def _():
        rt_ref[...] = jnp.zeros(rt_ref.shape, rt_ref.dtype)
        for k in range(hid):
            blockk = rtt_ref[k]
            for x in range(r4):
                rt_ref[k, x * cells:(x + 1) * cells, x * cells:(x + 1) * cells] = blockk

    qt = q_ref[...]
    for g in range(groups):
        @pl.when(g * GB < cnt_ref[t])
        def _():
            for slot in range(GB):
                blk_id = idx_ref[t, g * GB + slot]
                start = pl.multiple_of(blk_id * (br * cells), br * cells)
                corr = lax.dot_general(
                    qt, r_ref[pl.ds(start, br * cells), :], (((1,), (1,)), ((), ())),
                    preferred_element_type=jnp.float32,
                )
                c_scr[:, slot * br * cells:(slot + 1) * br * cells] = (corr / scale).astype(jnp.bfloat16)
            for p in range(nq):
                for c2 in range(2):
                    cc = c_scr[p * cells:(p + 1) * cells, c2 * CH:(c2 + 1) * CH]
                    for kg in range(hid // per):
                        hq = jnp.dot(
                            qt_ref[kg * per * cells:(kg + 1) * per * cells, :], cc,
                            preferred_element_type=jnp.float32,
                        )
                        hq = jnp.maximum(hq + bias_ref[kg * per * cells:(kg + 1) * per * cells, :], 0.0)
                        hq = hq.astype(jnp.bfloat16)
                        for kk in range(per):
                            k = kg * per + kk
                            row0 = (p * 2 + c2) * cells
                            h_scr[k, row0:row0 + cells, :] = hq[kk * cells:(kk + 1) * cells, :]
            f_scr[...] = jnp.dot(h_scr[0], rt_ref[0], preferred_element_type=jnp.float32)
            for k in range(1, hid):
                f_scr[...] += jnp.dot(h_scr[k], rt_ref[k], preferred_element_type=jnp.float32)
            for p in range(nq):
                acc = f_scr[p * 2 * cells:(p + 1) * 2 * cells, :]
                col_ref[0, p, 2 * g:2 * g + 2, :] = jnp.max(acc.reshape(2, cells, CH), axis=1)
                accT = acc.T
                row_ref[0, p, :, 2 * g * cells:(2 * g + 2) * cells] = jnp.max(
                    accT.reshape(r4, cells, 2 * cells), axis=1)


def local_scores(q_all, r_all, cand, query_table, ref_table, tap_bias):
    tiles = q_all.shape[0]
    depth = q_all.shape[2]
    nrl, cells = r_all.shape[0], r_all.shape[1]
    hid = query_table.shape[0]
    qt_per = 4
    nb = cand.shape[1]
    br = nrl // nb
    chunks = nrl * cells // CH
    r4 = CH // cells
    keep = (cand != 0).astype(jnp.int32)
    idx = jnp.argsort(1 - keep, axis=1, stable=True).astype(jnp.int32)
    cnt = jnp.sum(keep, axis=1).astype(jnp.int32)
    qstack = query_table.reshape(hid * cells, cells)
    bias_col = jnp.repeat(tap_bias.astype(jnp.float32), cells)[:, None]
    rtT = jnp.transpose(ref_table, (0, 2, 1))
    r2 = r_all.reshape(nrl * cells, depth)
    col, row = pl.pallas_call(
        filter_kernel,
        grid_spec=pltpu.PrefetchScalarGridSpec(
            num_scalar_prefetch=2,
            grid=(tiles,),
            in_specs=[
                pl.BlockSpec((None, qt_per * cells, depth), lambda t, i, c: (t, 0, 0)),
                pl.BlockSpec((nrl * cells, depth), lambda t, i, c: (0, 0)),
                pl.BlockSpec((hid * cells, cells), lambda t, i, c: (0, 0)),
                pl.BlockSpec((hid * cells, 1), lambda t, i, c: (0, 0)),
                pl.BlockSpec((hid, cells, cells), lambda t, i, c: (0, 0, 0)),
            ],
            out_specs=[
                pl.BlockSpec((1, qt_per, chunks, CH), lambda t, i, c: (t, 0, 0, 0)),
                pl.BlockSpec((1, qt_per, r4, chunks * cells), lambda t, i, c: (t, 0, 0, 0)),
            ],
            scratch_shapes=[
                pltpu.VMEM((qt_per * cells, GB * br * cells), jnp.bfloat16),
                pltpu.VMEM((hid, qt_per * 2 * cells, CH), jnp.bfloat16),
                pltpu.VMEM((hid, CH, CH), jnp.bfloat16),
                pltpu.VMEM((qt_per * 2 * cells, CH), jnp.float32),
            ],
        ),
        out_shape=[
            jax.ShapeDtypeStruct((tiles, qt_per, chunks, CH), jnp.float32),
            jax.ShapeDtypeStruct((tiles, qt_per, r4, chunks * cells), jnp.float32),
        ],
        compiler_params=pltpu.CompilerParams(vmem_limit_bytes=56 * 1024 * 1024),
    )(idx, cnt, q_all, r2, qstack, bias_col, rtT)
    col_pool = jnp.mean(col.reshape(tiles, qt_per, chunks, r4, cells), axis=-1)
    row_pool = jnp.mean(row.reshape(tiles, qt_per, r4, chunks, cells), axis=-1)
    row_pool = jnp.transpose(row_pool, (0, 1, 3, 2))
    packed = (0.5 * (row_pool + col_pool)).reshape(tiles, qt_per, nb, br)
    where_is = jnp.argsort(idx, axis=1)
    return jnp.take_along_axis(packed, where_is[:, None, :, None], axis=2)


def shards(queries, references, query_taps, ref_taps, tap_bias, candidates):
    query_table = conv_table(query_taps, SIDE)
    ref_table = conv_table(ref_taps, SIDE)
    blk = lax.axis_size("blk")
    wide = lax.axis_size("wide")
    me = lax.axis_index("blk")
    me_w = lax.axis_index("wide")
    query_unit = normalize(queries)
    qt_per, cells, depth = query_unit.shape
    pad = 16
    cand_rows = jnp.zeros((pad, depth), jnp.bfloat16).at[0, :candidates.shape[1]].set(
        candidates[0].astype(jnp.bfloat16))
    payload = jnp.concatenate([query_unit.reshape(qt_per * cells, depth), cand_rows], axis=0)
    q3 = lax.all_gather(payload, "blk", axis=0, tiled=False)
    cand = q3[:, qt_per * cells, :candidates.shape[1]]
    ref_unit = normalize(references)
    rl = ref_unit.shape[0]
    bits = wide.bit_length() - 1
    held = ref_unit
    for m in reversed(range(bits)):
        other = lax.ppermute(held, "wide", [(i, i ^ (1 << m)) for i in range(wide)])
        held = jnp.concatenate([held, other], axis=0)
    pos = jnp.arange(wide)
    rev = jnp.zeros_like(pos)
    for i in range(bits):
        rev = rev | (((pos >> i) & 1) << (bits - 1 - i))
    w_at = me_w ^ rev
    cand_pos = jnp.take(cand, w_at, axis=1)
    s = local_scores(q3, held, cand_pos, query_table, ref_table, tap_bias)
    p_of = jnp.argsort(w_at)
    s = jnp.take(s, p_of, axis=2)
    mine = lax.all_to_all(s, "blk", 0, 0, tiled=True)
    mine = jnp.transpose(mine, (1, 2, 0, 3)).reshape(qt_per, wide * blk * rl)
    block_refs = blk * rl
    keep = jnp.repeat(candidates[0] != 0, block_refs)
    return jnp.where(keep[None, :], mine, jnp.float32(0.0))


def solution(mesh):
    placed = (
        P(("wide", "blk"), None, None),
        P(("wide", "blk"), None, None),
        P(),
        P(),
        P(),
        P(("wide", "blk"), None),
    )
    return jax.shard_map(
        shards, mesh=mesh, in_specs=placed, out_specs=P(("wide", "blk"), None), check_vma=False
    )
```

```python
import math

import jax
import jax.numpy as jnp
from jax import lax
from jax.experimental import pallas as pl
from jax.experimental.pallas import tpu as pltpu
from jax.sharding import PartitionSpec as P

SIDE = 8


epsilon = 1e-06


def conv_table(weights, width):
    count = width * width
    position = jnp.arange(count, dtype=jnp.int32)
    grid_row = position // width
    grid_col = position % width
    delta_row = grid_row[None, :] - grid_row[:, None]
    delta_col = grid_col[None, :] - grid_col[:, None]
    inside = (jnp.abs(delta_row) <= 1) & (jnp.abs(delta_col) <= 1)
    tap_index = (delta_row + 1) * 3 + (delta_col + 1)
    selector = (tap_index[None] == jnp.arange(9, dtype=jnp.int32)[:, None, None]) & inside[None]
    table = jnp.sum(
        jnp.where(selector[None], weights.astype(jnp.float32)[:, :, None, None], jnp.float32(0.0)),
        axis=1,
    )
    return table.astype(jnp.bfloat16)


def normalize(features):
    values = features.astype(jnp.float32)
    inverse_rms = lax.rsqrt(jnp.mean(values * values, axis=-1, keepdims=True) + epsilon)
    return (values * inverse_rms).astype(jnp.bfloat16)


CH = 256


GB = 4


def filter_kernel(idx_ref, cnt_ref, q_ref, r_ref, qt_ref, bias_ref, rtt_ref, col_ref, row_ref,
                  c_scr, h_scr, rt_ref, f_scr):
    t = pl.program_id(0)
    rows = q_ref.shape[0]
    hid = rtt_ref.shape[0]
    cells = rtt_ref.shape[1]
    depth = q_ref.shape[1]
    nq = rows // cells
    r4 = CH // cells
    br = r4 // 2
    groups = col_ref.shape[2] // 2
    scale = math.sqrt(depth)
    per = hid // 4

    @pl.when(t == 0)
    def _():
        rt_ref[...] = jnp.zeros(rt_ref.shape, rt_ref.dtype)
        for k in range(hid):
            blockk = rtt_ref[k]
            for x in range(r4):
                rt_ref[k, x * cells:(x + 1) * cells, x * cells:(x + 1) * cells] = blockk

    qt = q_ref[...]
    for g in range(groups):
        @pl.when(g * GB < cnt_ref[t])
        def _():
            for slot in range(GB):
                blk_id = idx_ref[t, g * GB + slot]
                start = pl.multiple_of(blk_id * (br * cells), br * cells)
                corr = lax.dot_general(
                    qt, r_ref[pl.ds(start, br * cells), :], (((1,), (1,)), ((), ())),
                    preferred_element_type=jnp.float32,
                )
                c_scr[:, slot * br * cells:(slot + 1) * br * cells] = (corr / scale).astype(jnp.bfloat16)
            for p in range(nq):
                for c2 in range(2):
                    cc = c_scr[p * cells:(p + 1) * cells, c2 * CH:(c2 + 1) * CH]
                    for kg in range(hid // per):
                        hq = jnp.dot(
                            qt_ref[kg * per * cells:(kg + 1) * per * cells, :], cc,
                            preferred_element_type=jnp.float32,
                        )
                        hq = jnp.maximum(hq + bias_ref[kg * per * cells:(kg + 1) * per * cells, :], 0.0)
                        hq = hq.astype(jnp.bfloat16)
                        for kk in range(per):
                            k = kg * per + kk
                            row0 = (p * 2 + c2) * cells
                            h_scr[k, row0:row0 + cells, :] = hq[kk * cells:(kk + 1) * cells, :]
            f_scr[...] = jnp.dot(h_scr[0], rt_ref[0], preferred_element_type=jnp.float32)
            for k in range(1, hid):
                f_scr[...] += jnp.dot(h_scr[k], rt_ref[k], preferred_element_type=jnp.float32)
            for p in range(nq):
                acc = f_scr[p * 2 * cells:(p + 1) * 2 * cells, :]
                col_ref[0, p, 2 * g:2 * g + 2, :] = jnp.max(acc.reshape(2, cells, CH), axis=1)
                accT = acc.T
                row_ref[0, p, :, 2 * g * cells:(2 * g + 2) * cells] = jnp.max(
                    accT.reshape(r4, cells, 2 * cells), axis=1)


def local_scores(q_all, r_all, cand, query_table, ref_table, tap_bias):
    tiles = q_all.shape[0]
    depth = q_all.shape[2]
    nrl, cells = r_all.shape[0], r_all.shape[1]
    hid = query_table.shape[0]
    qt_per = 4
    nb = cand.shape[1]
    br = nrl // nb
    chunks = nrl * cells // CH
    r4 = CH // cells
    keep = (cand != 0).astype(jnp.int32)
    idx = jnp.argsort(1 - keep, axis=1, stable=True).astype(jnp.int32)
    cnt = jnp.sum(keep, axis=1).astype(jnp.int32)
    qstack = query_table.reshape(hid * cells, cells)
    bias_col = jnp.repeat(tap_bias.astype(jnp.float32), cells)[:, None]
    rtT = jnp.transpose(ref_table, (0, 2, 1))
    r2 = r_all.reshape(nrl * cells, depth)
    col, row = pl.pallas_call(
        filter_kernel,
        grid_spec=pltpu.PrefetchScalarGridSpec(
            num_scalar_prefetch=2,
            grid=(tiles,),
            in_specs=[
                pl.BlockSpec((None, qt_per * cells, depth), lambda t, i, c: (t, 0, 0)),
                pl.BlockSpec((nrl * cells, depth), lambda t, i, c: (0, 0)),
                pl.BlockSpec((hid * cells, cells), lambda t, i, c: (0, 0)),
                pl.BlockSpec((hid * cells, 1), lambda t, i, c: (0, 0)),
                pl.BlockSpec((hid, cells, cells), lambda t, i, c: (0, 0, 0)),
            ],
            out_specs=[
                pl.BlockSpec((1, qt_per, chunks, CH), lambda t, i, c: (t, 0, 0, 0)),
                pl.BlockSpec((1, qt_per, r4, chunks * cells), lambda t, i, c: (t, 0, 0, 0)),
            ],
            scratch_shapes=[
                pltpu.VMEM((qt_per * cells, GB * br * cells), jnp.bfloat16),
                pltpu.VMEM((hid, qt_per * 2 * cells, CH), jnp.bfloat16),
                pltpu.VMEM((hid, CH, CH), jnp.bfloat16),
                pltpu.VMEM((qt_per * 2 * cells, CH), jnp.float32),
            ],
        ),
        out_shape=[
            jax.ShapeDtypeStruct((tiles, qt_per, chunks, CH), jnp.float32),
            jax.ShapeDtypeStruct((tiles, qt_per, r4, chunks * cells), jnp.float32),
        ],
        compiler_params=pltpu.CompilerParams(vmem_limit_bytes=56 * 1024 * 1024),
    )(idx, cnt, q_all, r2, qstack, bias_col, rtT)
    col_pool = jnp.mean(col.reshape(tiles, qt_per, chunks, r4, cells), axis=-1)
    row_pool = jnp.mean(row.reshape(tiles, qt_per, r4, chunks, cells), axis=-1)
    row_pool = jnp.transpose(row_pool, (0, 1, 3, 2))
    packed = (0.5 * (row_pool + col_pool)).reshape(tiles, qt_per, nb, br)
    where_is = jnp.argsort(idx, axis=1)
    return jnp.take_along_axis(packed, where_is[:, None, :, None], axis=2)


def doubling(x, axis, size):
    bits = size.bit_length() - 1
    for m in reversed(range(bits)):
        other = lax.ppermute(x, axis, [(i, i ^ (1 << m)) for i in range(size)])
        x = jnp.concatenate([x, other], axis=0)
    return x


def bit_reverse(size):
    bits = size.bit_length() - 1
    pos = jnp.arange(size)
    rev = jnp.zeros_like(pos)
    for i in range(bits):
        rev = rev | (((pos >> i) & 1) << (bits - 1 - i))
    return rev


def shards(queries, references, query_taps, ref_taps, tap_bias, candidates):
    query_table = conv_table(query_taps, SIDE)
    ref_table = conv_table(ref_taps, SIDE)
    blk = lax.axis_size("blk")
    wide = lax.axis_size("wide")
    me = lax.axis_index("blk")
    me_w = lax.axis_index("wide")
    query_unit = normalize(queries)
    qt_per, cells, depth = query_unit.shape
    pad = 16
    cand_rows = jnp.zeros((pad, depth), jnp.bfloat16).at[0, :candidates.shape[1]].set(
        candidates[0].astype(jnp.bfloat16))
    payload = jnp.concatenate([query_unit.reshape(qt_per * cells, depth), cand_rows], axis=0)
    q3 = doubling(payload[None], "blk", blk)
    cand = q3[:, qt_per * cells, :candidates.shape[1]]
    b_at = me ^ bit_reverse(blk)
    ref_unit = normalize(references)
    rl = ref_unit.shape[0]
    held = doubling(ref_unit, "wide", wide)
    w_at = me_w ^ bit_reverse(wide)
    cand_pos = jnp.take(cand, w_at, axis=1)
    s = local_scores(q3, held, cand_pos, query_table, ref_table, tap_bias)
    p_of = jnp.argsort(w_at)
    s = jnp.take(s, p_of, axis=2)
    s = jnp.take(s, jnp.argsort(b_at), axis=0)
    mine = lax.all_to_all(s, "blk", 0, 0, tiled=True)
    mine = jnp.transpose(mine, (1, 2, 0, 3)).reshape(qt_per, wide * blk * rl)
    block_refs = blk * rl
    keep = jnp.repeat(candidates[0] != 0, block_refs)
    return jnp.where(keep[None, :], mine, jnp.float32(0.0))


def solution(mesh):
    placed = (
        P(("wide", "blk"), None, None),
        P(("wide", "blk"), None, None),
        P(),
        P(),
        P(),
        P(("wide", "blk"), None),
    )
    return jax.shard_map(
        shards, mesh=mesh, in_specs=placed, out_specs=P(("wide", "blk"), None), check_vma=False
    )
```

```python
import math

import jax
import jax.numpy as jnp
from jax import lax
from jax.experimental import pallas as pl
from jax.experimental.pallas import tpu as pltpu
from jax.sharding import PartitionSpec as P

SIDE = 8


epsilon = 1e-06


def conv_table(weights, width):
    count = width * width
    position = jnp.arange(count, dtype=jnp.int32)
    grid_row = position // width
    grid_col = position % width
    delta_row = grid_row[None, :] - grid_row[:, None]
    delta_col = grid_col[None, :] - grid_col[:, None]
    inside = (jnp.abs(delta_row) <= 1) & (jnp.abs(delta_col) <= 1)
    tap_index = (delta_row + 1) * 3 + (delta_col + 1)
    selector = (tap_index[None] == jnp.arange(9, dtype=jnp.int32)[:, None, None]) & inside[None]
    table = jnp.sum(
        jnp.where(selector[None], weights.astype(jnp.float32)[:, :, None, None], jnp.float32(0.0)),
        axis=1,
    )
    return table.astype(jnp.bfloat16)


def normalize(features):
    values = features.astype(jnp.float32)
    inverse_rms = lax.rsqrt(jnp.mean(values * values, axis=-1, keepdims=True) + epsilon)
    return (values * inverse_rms).astype(jnp.bfloat16)


CH = 256


GB = 4


def filter_kernel(idx_ref, cnt_ref, q_ref, r_ref, qt_ref, bias_ref, rtt_ref, col_ref, row_ref,
                  c_scr, h_scr, rt_ref, f_scr):
    t = pl.program_id(0)
    rows = q_ref.shape[0]
    hid = rtt_ref.shape[0]
    cells = rtt_ref.shape[1]
    depth = q_ref.shape[1]
    nq = rows // cells
    r4 = CH // cells
    br = r4 // 2
    groups = col_ref.shape[2] // 2
    scale = math.sqrt(depth)
    per = hid // 4

    @pl.when(t == 0)
    def _():
        rt_ref[...] = jnp.zeros(rt_ref.shape, rt_ref.dtype)
        for k in range(hid):
            blockk = rtt_ref[k]
            for x in range(r4):
                rt_ref[k, x * cells:(x + 1) * cells, x * cells:(x + 1) * cells] = blockk

    qt = q_ref[...]
    for g in range(groups):
        @pl.when(g * GB < cnt_ref[t])
        def _():
            for slot in range(GB):
                blk_id = idx_ref[t, g * GB + slot]
                start = pl.multiple_of(blk_id * (br * cells), br * cells)
                corr = lax.dot_general(
                    qt, r_ref[pl.ds(start, br * cells), :], (((1,), (1,)), ((), ())),
                    preferred_element_type=jnp.float32,
                )
                c_scr[:, slot * br * cells:(slot + 1) * br * cells] = (corr / scale).astype(jnp.bfloat16)
            for p in range(nq):
                for c2 in range(2):
                    cc = c_scr[p * cells:(p + 1) * cells, c2 * CH:(c2 + 1) * CH]
                    for kg in range(hid // per):
                        hq = jnp.dot(
                            qt_ref[kg * per * cells:(kg + 1) * per * cells, :], cc,
                            preferred_element_type=jnp.float32,
                        )
                        hq = jnp.maximum(hq + bias_ref[kg * per * cells:(kg + 1) * per * cells, :], 0.0)
                        hq = hq.astype(jnp.bfloat16)
                        for kk in range(per):
                            k = kg * per + kk
                            row0 = (p * 2 + c2) * cells
                            h_scr[k, row0:row0 + cells, :] = hq[kk * cells:(kk + 1) * cells, :]
            f_scr[...] = jnp.dot(h_scr[0], rt_ref[0], preferred_element_type=jnp.float32)
            for k in range(1, hid):
                f_scr[...] += jnp.dot(h_scr[k], rt_ref[k], preferred_element_type=jnp.float32)
            for p in range(nq):
                acc = f_scr[p * 2 * cells:(p + 1) * 2 * cells, :]
                col_ref[0, p, 2 * g:2 * g + 2, :] = jnp.max(acc.reshape(2, cells, CH), axis=1)
                accT = acc.T
                row_ref[0, p, :, 2 * g * cells:(2 * g + 2) * cells] = jnp.max(
                    accT.reshape(r4, cells, 2 * cells), axis=1)


def local_scores(q_all, r_all, cand, query_table, ref_table, tap_bias):
    tiles = q_all.shape[0]
    depth = q_all.shape[2]
    nrl, cells = r_all.shape[0], r_all.shape[1]
    hid = query_table.shape[0]
    qt_per = 4
    nb = cand.shape[1]
    br = nrl // nb
    chunks = nrl * cells // CH
    r4 = CH // cells
    keep = (cand != 0).astype(jnp.int32)
    idx = jnp.argsort(1 - keep, axis=1, stable=True).astype(jnp.int32)
    cnt = jnp.sum(keep, axis=1).astype(jnp.int32)
    qstack = query_table.reshape(hid * cells, cells)
    bias_col = jnp.repeat(tap_bias.astype(jnp.float32), cells)[:, None]
    rtT = jnp.transpose(ref_table, (0, 2, 1))
    r2 = r_all.reshape(nrl * cells, depth)
    col, row = pl.pallas_call(
        filter_kernel,
        grid_spec=pltpu.PrefetchScalarGridSpec(
            num_scalar_prefetch=2,
            grid=(tiles,),
            in_specs=[
                pl.BlockSpec((None, qt_per * cells, depth), lambda t, i, c: (t, 0, 0)),
                pl.BlockSpec((nrl * cells, depth), lambda t, i, c: (0, 0)),
                pl.BlockSpec((hid * cells, cells), lambda t, i, c: (0, 0)),
                pl.BlockSpec((hid * cells, 1), lambda t, i, c: (0, 0)),
                pl.BlockSpec((hid, cells, cells), lambda t, i, c: (0, 0, 0)),
            ],
            out_specs=[
                pl.BlockSpec((1, qt_per, chunks, CH), lambda t, i, c: (t, 0, 0, 0)),
                pl.BlockSpec((1, qt_per, r4, chunks * cells), lambda t, i, c: (t, 0, 0, 0)),
            ],
            scratch_shapes=[
                pltpu.VMEM((qt_per * cells, GB * br * cells), jnp.bfloat16),
                pltpu.VMEM((hid, qt_per * 2 * cells, CH), jnp.bfloat16),
                pltpu.VMEM((hid, CH, CH), jnp.bfloat16),
                pltpu.VMEM((qt_per * 2 * cells, CH), jnp.float32),
            ],
        ),
        out_shape=[
            jax.ShapeDtypeStruct((tiles, qt_per, chunks, CH), jnp.float32),
            jax.ShapeDtypeStruct((tiles, qt_per, r4, chunks * cells), jnp.float32),
        ],
        compiler_params=pltpu.CompilerParams(vmem_limit_bytes=56 * 1024 * 1024),
    )(idx, cnt, q_all, r2, qstack, bias_col, rtT)
    col_pool = jnp.mean(col.reshape(tiles, qt_per, chunks, r4, cells), axis=-1)
    row_pool = jnp.mean(row.reshape(tiles, qt_per, r4, chunks, cells), axis=-1)
    row_pool = jnp.transpose(row_pool, (0, 1, 3, 2))
    packed = (0.5 * (row_pool + col_pool)).reshape(tiles, qt_per, nb, br)
    where_is = jnp.argsort(idx, axis=1)
    return jnp.take_along_axis(packed, where_is[:, None, :, None], axis=2)


def doubling(x, axis, size):
    bits = size.bit_length() - 1
    for m in reversed(range(bits)):
        pairs = [(i, i ^ (1 << m)) for i in range(size)]
        if x.shape[0] >= 4:
            half = x.shape[0] // 2
            other = [lax.ppermute(x[:half], axis, pairs), lax.ppermute(x[half:], axis, pairs)]
        else:
            other = [lax.ppermute(x, axis, pairs)]
        x = jnp.concatenate([x] + other, axis=0)
    return x


def bit_reverse(size):
    bits = size.bit_length() - 1
    pos = jnp.arange(size)
    rev = jnp.zeros_like(pos)
    for i in range(bits):
        rev = rev | (((pos >> i) & 1) << (bits - 1 - i))
    return rev


def shards(queries, references, query_taps, ref_taps, tap_bias, candidates):
    query_table = conv_table(query_taps, SIDE)
    ref_table = conv_table(ref_taps, SIDE)
    blk = lax.axis_size("blk")
    wide = lax.axis_size("wide")
    me = lax.axis_index("blk")
    me_w = lax.axis_index("wide")
    query_unit = normalize(queries)
    qt_per, cells, depth = query_unit.shape
    pad = 16
    cand_rows = jnp.zeros((pad, depth), jnp.bfloat16).at[0, :candidates.shape[1]].set(
        candidates[0].astype(jnp.bfloat16))
    payload = jnp.concatenate([query_unit.reshape(qt_per * cells, depth), cand_rows], axis=0)
    q3 = doubling(payload[None], "blk", blk)
    cand = q3[:, qt_per * cells, :candidates.shape[1]]
    b_at = me ^ bit_reverse(blk)
    ref_unit = normalize(references)
    rl = ref_unit.shape[0]
    held = doubling(ref_unit, "wide", wide)
    w_at = me_w ^ bit_reverse(wide)
    cand_pos = jnp.take(cand, w_at, axis=1)
    s = local_scores(q3, held, cand_pos, query_table, ref_table, tap_bias)
    p_of = jnp.argsort(w_at)
    s = jnp.take(s, p_of, axis=2)
    s = jnp.take(s, jnp.argsort(b_at), axis=0)
    mine = lax.all_to_all(s, "blk", 0, 0, tiled=True)
    mine = jnp.transpose(mine, (1, 2, 0, 3)).reshape(qt_per, wide * blk * rl)
    block_refs = blk * rl
    keep = jnp.repeat(candidates[0] != 0, block_refs)
    return jnp.where(keep[None, :], mine, jnp.float32(0.0))


def solution(mesh):
    placed = (
        P(("wide", "blk"), None, None),
        P(("wide", "blk"), None, None),
        P(),
        P(),
        P(),
        P(("wide", "blk"), None),
    )
    return jax.shard_map(
        shards, mesh=mesh, in_specs=placed, out_specs=P(("wide", "blk"), None), check_vma=False
    )
```

```python
import math

import jax
import jax.numpy as jnp
from jax import lax
from jax.experimental import pallas as pl
from jax.experimental.pallas import tpu as pltpu
from jax.sharding import PartitionSpec as P

SIDE = 8


epsilon = 1e-06


def conv_table(weights, width):
    count = width * width
    position = jnp.arange(count, dtype=jnp.int32)
    grid_row = position // width
    grid_col = position % width
    delta_row = grid_row[None, :] - grid_row[:, None]
    delta_col = grid_col[None, :] - grid_col[:, None]
    inside = (jnp.abs(delta_row) <= 1) & (jnp.abs(delta_col) <= 1)
    tap_index = (delta_row + 1) * 3 + (delta_col + 1)
    selector = (tap_index[None] == jnp.arange(9, dtype=jnp.int32)[:, None, None]) & inside[None]
    table = jnp.sum(
        jnp.where(selector[None], weights.astype(jnp.float32)[:, :, None, None], jnp.float32(0.0)),
        axis=1,
    )
    return table.astype(jnp.bfloat16)


def normalize(features):
    values = features.astype(jnp.float32)
    inverse_rms = lax.rsqrt(jnp.mean(values * values, axis=-1, keepdims=True) + epsilon)
    return (values * inverse_rms).astype(jnp.bfloat16)


CH = 256


GB = 4


def filter_kernel(idx_ref, cnt_ref, q_ref, r_ref, qt_ref, bias_ref, rtt_ref, col_ref, row_ref,
                  c_scr, h_scr, rt_ref, f_scr):
    t = pl.program_id(0)
    rows = q_ref.shape[0]
    hid = rtt_ref.shape[0]
    cells = rtt_ref.shape[1]
    depth = q_ref.shape[1]
    nq = rows // cells
    r4 = CH // cells
    br = r4 // 2
    groups = col_ref.shape[2] // 2
    scale = math.sqrt(depth)
    per = hid // 4

    @pl.when(t == 0)
    def _():
        rt_ref[...] = jnp.zeros(rt_ref.shape, rt_ref.dtype)
        for k in range(hid):
            blockk = rtt_ref[k]
            for x in range(r4):
                rt_ref[k, x * cells:(x + 1) * cells, x * cells:(x + 1) * cells] = blockk

    qt = q_ref[...]
    for g in range(groups):
        @pl.when(g * GB < cnt_ref[t])
        def _():
            for slot in range(GB):
                blk_id = idx_ref[t, g * GB + slot]
                start = pl.multiple_of(blk_id * (br * cells), br * cells)
                corr = lax.dot_general(
                    qt, r_ref[pl.ds(start, br * cells), :], (((1,), (1,)), ((), ())),
                    preferred_element_type=jnp.float32,
                )
                c_scr[:, slot * br * cells:(slot + 1) * br * cells] = (corr / scale).astype(jnp.bfloat16)
            for p in range(nq):
                for c2 in range(2):
                    cc = c_scr[p * cells:(p + 1) * cells, c2 * CH:(c2 + 1) * CH]
                    for kg in range(hid // per):
                        hq = jnp.dot(
                            qt_ref[kg * per * cells:(kg + 1) * per * cells, :], cc,
                            preferred_element_type=jnp.float32,
                        )
                        hq = jnp.maximum(hq + bias_ref[kg * per * cells:(kg + 1) * per * cells, :], 0.0)
                        hq = hq.astype(jnp.bfloat16)
                        for kk in range(per):
                            k = kg * per + kk
                            row0 = (p * 2 + c2) * cells
                            h_scr[k, row0:row0 + cells, :] = hq[kk * cells:(kk + 1) * cells, :]
            f_scr[...] = jnp.dot(h_scr[0], rt_ref[0], preferred_element_type=jnp.float32)
            for k in range(1, hid):
                f_scr[...] += jnp.dot(h_scr[k], rt_ref[k], preferred_element_type=jnp.float32)
            for p in range(nq):
                acc = f_scr[p * 2 * cells:(p + 1) * 2 * cells, :]
                col_ref[0, p, 2 * g:2 * g + 2, :] = jnp.max(acc.reshape(2, cells, CH), axis=1)
                accT = acc.T
                row_ref[0, p, :, 2 * g * cells:(2 * g + 2) * cells] = jnp.max(
                    accT.reshape(r4, cells, 2 * cells), axis=1)


def local_scores(q_all, r_all, cand, query_table, ref_table, tap_bias):
    tiles = q_all.shape[0]
    depth = q_all.shape[2]
    nrl, cells = r_all.shape[0], r_all.shape[1]
    hid = query_table.shape[0]
    qt_per = 4
    nb = cand.shape[1]
    br = nrl // nb
    chunks = nrl * cells // CH
    r4 = CH // cells
    keep = (cand != 0).astype(jnp.int32)
    idx = jnp.argsort(1 - keep, axis=1, stable=True).astype(jnp.int32)
    cnt = jnp.sum(keep, axis=1).astype(jnp.int32)
    qstack = query_table.reshape(hid * cells, cells)
    bias_col = jnp.repeat(tap_bias.astype(jnp.float32), cells)[:, None]
    rtT = jnp.transpose(ref_table, (0, 2, 1))
    r2 = r_all.reshape(nrl * cells, depth)
    col, row = pl.pallas_call(
        filter_kernel,
        grid_spec=pltpu.PrefetchScalarGridSpec(
            num_scalar_prefetch=2,
            grid=(tiles,),
            in_specs=[
                pl.BlockSpec((None, qt_per * cells, depth), lambda t, i, c: (t, 0, 0)),
                pl.BlockSpec((nrl * cells, depth), lambda t, i, c: (0, 0)),
                pl.BlockSpec((hid * cells, cells), lambda t, i, c: (0, 0)),
                pl.BlockSpec((hid * cells, 1), lambda t, i, c: (0, 0)),
                pl.BlockSpec((hid, cells, cells), lambda t, i, c: (0, 0, 0)),
            ],
            out_specs=[
                pl.BlockSpec((1, qt_per, chunks, CH), lambda t, i, c: (t, 0, 0, 0)),
                pl.BlockSpec((1, qt_per, r4, chunks * cells), lambda t, i, c: (t, 0, 0, 0)),
            ],
            scratch_shapes=[
                pltpu.VMEM((qt_per * cells, GB * br * cells), jnp.bfloat16),
                pltpu.VMEM((hid, qt_per * 2 * cells, CH), jnp.bfloat16),
                pltpu.VMEM((hid, CH, CH), jnp.bfloat16),
                pltpu.VMEM((qt_per * 2 * cells, CH), jnp.float32),
            ],
        ),
        out_shape=[
            jax.ShapeDtypeStruct((tiles, qt_per, chunks, CH), jnp.float32),
            jax.ShapeDtypeStruct((tiles, qt_per, r4, chunks * cells), jnp.float32),
        ],
        compiler_params=pltpu.CompilerParams(vmem_limit_bytes=56 * 1024 * 1024),
    )(idx, cnt, q_all, r2, qstack, bias_col, rtT)
    hi = lax.Precision.HIGHEST
    avg_c = (jnp.arange(CH)[:, None] // cells == jnp.arange(r4)[None, :]).astype(jnp.float32) / cells
    col_pool = jnp.einsum("tpcl,lr->tpcr", col, avg_c, precision=hi)
    avg_r = (jnp.arange(chunks * cells)[:, None] // cells == jnp.arange(chunks)[None, :]).astype(
        jnp.float32) / cells
    row_pool = jnp.einsum("tprl,lc->tprc", row, avg_r, precision=hi)
    row_pool = jnp.transpose(row_pool, (0, 1, 3, 2))
    packed = (0.5 * (row_pool + col_pool)).reshape(tiles, qt_per, nb, br)
    where_is = jnp.argsort(idx, axis=1)
    return jnp.take_along_axis(packed, where_is[:, None, :, None], axis=2)


def doubling(x, axis, size):
    bits = size.bit_length() - 1
    for m in reversed(range(bits)):
        other = lax.ppermute(x, axis, [(i, i ^ (1 << m)) for i in range(size)])
        x = jnp.concatenate([x, other], axis=0)
    return x


def bit_reverse(size):
    bits = size.bit_length() - 1
    pos = jnp.arange(size)
    rev = jnp.zeros_like(pos)
    for i in range(bits):
        rev = rev | (((pos >> i) & 1) << (bits - 1 - i))
    return rev


def shards(queries, references, query_taps, ref_taps, tap_bias, candidates):
    query_table = conv_table(query_taps, SIDE)
    ref_table = conv_table(ref_taps, SIDE)
    blk = lax.axis_size("blk")
    wide = lax.axis_size("wide")
    me = lax.axis_index("blk")
    me_w = lax.axis_index("wide")
    query_unit = normalize(queries)
    qt_per, cells, depth = query_unit.shape
    pad = 16
    cand_rows = jnp.zeros((pad, depth), jnp.bfloat16).at[0, :candidates.shape[1]].set(
        candidates[0].astype(jnp.bfloat16))
    payload = jnp.concatenate([query_unit.reshape(qt_per * cells, depth), cand_rows], axis=0)
    q3 = doubling(payload[None], "blk", blk)
    cand = q3[:, qt_per * cells, :candidates.shape[1]]
    b_at = me ^ bit_reverse(blk)
    ref_unit = normalize(references)
    rl = ref_unit.shape[0]
    held = doubling(ref_unit, "wide", wide)
    w_at = me_w ^ bit_reverse(wide)
    cand_pos = jnp.take(cand, w_at, axis=1)
    s = local_scores(q3, held, cand_pos, query_table, ref_table, tap_bias)
    p_of = jnp.argsort(w_at)
    s = jnp.take(s, p_of, axis=2)
    s = jnp.take(s, jnp.argsort(b_at), axis=0)
    mine = lax.all_to_all(s, "blk", 0, 0, tiled=True)
    mine = jnp.transpose(mine, (1, 2, 0, 3)).reshape(qt_per, wide * blk * rl)
    block_refs = blk * rl
    keep = jnp.repeat(candidates[0] != 0, block_refs)
    return jnp.where(keep[None, :], mine, jnp.float32(0.0))


def solution(mesh):
    placed = (
        P(("wide", "blk"), None, None),
        P(("wide", "blk"), None, None),
        P(),
        P(),
        P(),
        P(("wide", "blk"), None),
    )
    return jax.shard_map(
        shards, mesh=mesh, in_specs=placed, out_specs=P(("wide", "blk"), None), check_vma=False
    )
```

```python
import math

import jax
import jax.numpy as jnp
from jax import lax
from jax.experimental import pallas as pl
from jax.experimental.pallas import tpu as pltpu
from jax.sharding import PartitionSpec as P

SIDE = 8


epsilon = 1e-06


def conv_table(weights, width):
    count = width * width
    position = jnp.arange(count, dtype=jnp.int32)
    grid_row = position // width
    grid_col = position % width
    delta_row = grid_row[None, :] - grid_row[:, None]
    delta_col = grid_col[None, :] - grid_col[:, None]
    inside = (jnp.abs(delta_row) <= 1) & (jnp.abs(delta_col) <= 1)
    tap_index = (delta_row + 1) * 3 + (delta_col + 1)
    selector = (tap_index[None] == jnp.arange(9, dtype=jnp.int32)[:, None, None]) & inside[None]
    table = jnp.sum(
        jnp.where(selector[None], weights.astype(jnp.float32)[:, :, None, None], jnp.float32(0.0)),
        axis=1,
    )
    return table.astype(jnp.bfloat16)


def normalize(features):
    values = features.astype(jnp.float32)
    inverse_rms = lax.rsqrt(jnp.mean(values * values, axis=-1, keepdims=True) + epsilon)
    return (values * inverse_rms).astype(jnp.bfloat16)


CH = 256


GB = 4


def filter_kernel(idx_ref, cnt_ref, q_ref, r_ref, qt_ref, bias_ref, rtt_ref, col_ref, row_ref,
                  c_scr, h_scr, rt_ref, f_scr):
    t = pl.program_id(0)
    rows = q_ref.shape[0]
    hid = rtt_ref.shape[0]
    cells = rtt_ref.shape[1]
    depth = q_ref.shape[1]
    nq = rows // cells
    r4 = CH // cells
    br = r4 // 2
    groups = col_ref.shape[2] // 2
    scale = math.sqrt(depth)
    per = hid // 4

    @pl.when(t == 0)
    def _():
        rt_ref[...] = jnp.zeros(rt_ref.shape, rt_ref.dtype)
        for k in range(hid):
            blockk = rtt_ref[k]
            for x in range(r4):
                rt_ref[k, x * cells:(x + 1) * cells, x * cells:(x + 1) * cells] = blockk

    qt = q_ref[...]
    for g in range(groups):
        @pl.when(g * GB < cnt_ref[t])
        def _():
            for slot in range(GB):
                blk_id = idx_ref[t, g * GB + slot]
                start = pl.multiple_of(blk_id * (br * cells), br * cells)
                corr = lax.dot_general(
                    qt, r_ref[pl.ds(start, br * cells), :], (((1,), (1,)), ((), ())),
                    preferred_element_type=jnp.float32,
                )
                c_scr[:, slot * br * cells:(slot + 1) * br * cells] = (corr / scale).astype(jnp.bfloat16)
            for p in range(nq):
                for c2 in range(2):
                    cc = c_scr[p * cells:(p + 1) * cells, c2 * CH:(c2 + 1) * CH]
                    for kg in range(hid // per):
                        hq = jnp.dot(
                            qt_ref[kg * per * cells:(kg + 1) * per * cells, :], cc,
                            preferred_element_type=jnp.float32,
                        )
                        hq = jnp.maximum(hq + bias_ref[kg * per * cells:(kg + 1) * per * cells, :], 0.0)
                        hq = hq.astype(jnp.bfloat16)
                        for kk in range(per):
                            k = kg * per + kk
                            row0 = (p * 2 + c2) * cells
                            h_scr[k, row0:row0 + cells, :] = hq[kk * cells:(kk + 1) * cells, :]
            f_scr[...] = jnp.dot(h_scr[0], rt_ref[0], preferred_element_type=jnp.float32)
            for k in range(1, hid):
                f_scr[...] += jnp.dot(h_scr[k], rt_ref[k], preferred_element_type=jnp.float32)
            for p in range(nq):
                acc = f_scr[p * 2 * cells:(p + 1) * 2 * cells, :]
                col_ref[0, p, 2 * g:2 * g + 2, :] = jnp.max(acc.reshape(2, cells, CH), axis=1)
                accT = acc.T
                row_ref[0, p, :, 2 * g * cells:(2 * g + 2) * cells] = jnp.max(
                    accT.reshape(r4, cells, 2 * cells), axis=1)


def local_scores(q_all, r_all, cand, query_table, ref_table, tap_bias):
    tiles = q_all.shape[0]
    depth = q_all.shape[2]
    nrl, cells = r_all.shape[0], r_all.shape[1]
    hid = query_table.shape[0]
    qt_per = 4
    nb = cand.shape[1]
    br = nrl // nb
    chunks = nrl * cells // CH
    r4 = CH // cells
    keep = (cand != 0).astype(jnp.int32)
    idx = jnp.argsort(1 - keep, axis=1, stable=True).astype(jnp.int32)
    cnt = jnp.sum(keep, axis=1).astype(jnp.int32)
    qstack = query_table.reshape(hid * cells, cells)
    bias_col = jnp.repeat(tap_bias.astype(jnp.float32), cells)[:, None]
    rtT = jnp.transpose(ref_table, (0, 2, 1))
    r2 = r_all.reshape(nrl * cells, depth)
    col, row = pl.pallas_call(
        filter_kernel,
        grid_spec=pltpu.PrefetchScalarGridSpec(
            num_scalar_prefetch=2,
            grid=(tiles,),
            in_specs=[
                pl.BlockSpec((None, qt_per * cells, depth), lambda t, i, c: (t, 0, 0)),
                pl.BlockSpec((nrl * cells, depth), lambda t, i, c: (0, 0)),
                pl.BlockSpec((hid * cells, cells), lambda t, i, c: (0, 0)),
                pl.BlockSpec((hid * cells, 1), lambda t, i, c: (0, 0)),
                pl.BlockSpec((hid, cells, cells), lambda t, i, c: (0, 0, 0)),
            ],
            out_specs=[
                pl.BlockSpec((1, qt_per, chunks, CH), lambda t, i, c: (t, 0, 0, 0)),
                pl.BlockSpec((1, qt_per, r4, chunks * cells), lambda t, i, c: (t, 0, 0, 0)),
            ],
            scratch_shapes=[
                pltpu.VMEM((qt_per * cells, GB * br * cells), jnp.bfloat16),
                pltpu.VMEM((hid, qt_per * 2 * cells, CH), jnp.bfloat16),
                pltpu.VMEM((hid, CH, CH), jnp.bfloat16),
                pltpu.VMEM((qt_per * 2 * cells, CH), jnp.float32),
            ],
        ),
        out_shape=[
            jax.ShapeDtypeStruct((tiles, qt_per, chunks, CH), jnp.float32),
            jax.ShapeDtypeStruct((tiles, qt_per, r4, chunks * cells), jnp.float32),
        ],
        compiler_params=pltpu.CompilerParams(vmem_limit_bytes=56 * 1024 * 1024),
    )(idx, cnt, q_all, r2, qstack, bias_col, rtT)
    hi = lax.Precision.HIGHEST
    avg_c = (jnp.arange(CH)[:, None] // cells == jnp.arange(r4)[None, :]).astype(jnp.float32) / cells
    col_pool = jnp.einsum("tpcl,lr->tpcr", col, avg_c, precision=hi)
    avg_r = (jnp.arange(chunks * cells)[:, None] // cells == jnp.arange(chunks)[None, :]).astype(
        jnp.float32) / cells
    row_pool = jnp.einsum("tprl,lc->tprc", row, avg_r, precision=hi)
    row_pool = jnp.transpose(row_pool, (0, 1, 3, 2))
    packed = (0.5 * (row_pool + col_pool)).reshape(tiles, qt_per, nb, br)
    where_is = jnp.argsort(idx, axis=1)
    return packed, where_is


def doubling(x, axis, size):
    bits = size.bit_length() - 1
    for m in reversed(range(bits)):
        other = lax.ppermute(x, axis, [(i, i ^ (1 << m)) for i in range(size)])
        x = jnp.concatenate([x, other], axis=0)
    return x


def bit_reverse(size):
    bits = size.bit_length() - 1
    pos = jnp.arange(size)
    rev = jnp.zeros_like(pos)
    for i in range(bits):
        rev = rev | (((pos >> i) & 1) << (bits - 1 - i))
    return rev


def shards(queries, references, query_taps, ref_taps, tap_bias, candidates):
    query_table = conv_table(query_taps, SIDE)
    ref_table = conv_table(ref_taps, SIDE)
    blk = lax.axis_size("blk")
    wide = lax.axis_size("wide")
    me = lax.axis_index("blk")
    me_w = lax.axis_index("wide")
    query_unit = normalize(queries)
    qt_per, cells, depth = query_unit.shape
    pad = 16
    cand_rows = jnp.zeros((pad, depth), jnp.bfloat16).at[0, :candidates.shape[1]].set(
        candidates[0].astype(jnp.bfloat16))
    payload = jnp.concatenate([query_unit.reshape(qt_per * cells, depth), cand_rows], axis=0)
    q3 = doubling(payload[None], "blk", blk)
    cand = q3[:, qt_per * cells, :candidates.shape[1]]
    b_at = me ^ bit_reverse(blk)
    ref_unit = normalize(references)
    rl = ref_unit.shape[0]
    held = doubling(ref_unit, "wide", wide)
    w_at = me_w ^ bit_reverse(wide)
    cand_pos = jnp.take(cand, w_at, axis=1)
    packed, where_is = local_scores(q3, held, cand_pos, query_table, ref_table, tap_bias)
    p_of = jnp.argsort(w_at)
    t_of = jnp.argsort(b_at)
    g = jnp.take(where_is[t_of], p_of, axis=1)
    s = packed[t_of[:, None], :, g, :]
    s = jnp.transpose(s, (0, 2, 1, 3))
    mine = lax.all_to_all(s, "blk", 0, 0, tiled=True)
    mine = jnp.transpose(mine, (1, 2, 0, 3)).reshape(qt_per, wide * blk * rl)
    block_refs = blk * rl
    keep = jnp.repeat(candidates[0] != 0, block_refs)
    return jnp.where(keep[None, :], mine, jnp.float32(0.0))


def solution(mesh):
    placed = (
        P(("wide", "blk"), None, None),
        P(("wide", "blk"), None, None),
        P(),
        P(),
        P(),
        P(("wide", "blk"), None),
    )
    return jax.shard_map(
        shards, mesh=mesh, in_specs=placed, out_specs=P(("wide", "blk"), None), check_vma=False
    )
```

```python
import math

import jax
import jax.numpy as jnp
from jax import lax
from jax.experimental import pallas as pl
from jax.experimental.pallas import tpu as pltpu
from jax.sharding import PartitionSpec as P

SIDE = 8


epsilon = 1e-06


def conv_table(weights, width):
    count = width * width
    position = jnp.arange(count, dtype=jnp.int32)
    grid_row = position // width
    grid_col = position % width
    delta_row = grid_row[None, :] - grid_row[:, None]
    delta_col = grid_col[None, :] - grid_col[:, None]
    inside = (jnp.abs(delta_row) <= 1) & (jnp.abs(delta_col) <= 1)
    tap_index = (delta_row + 1) * 3 + (delta_col + 1)
    selector = (tap_index[None] == jnp.arange(9, dtype=jnp.int32)[:, None, None]) & inside[None]
    table = jnp.sum(
        jnp.where(selector[None], weights.astype(jnp.float32)[:, :, None, None], jnp.float32(0.0)),
        axis=1,
    )
    return table.astype(jnp.bfloat16)


def normalize(features):
    values = features.astype(jnp.float32)
    inverse_rms = lax.rsqrt(jnp.mean(values * values, axis=-1, keepdims=True) + epsilon)
    return (values * inverse_rms).astype(jnp.bfloat16)


CH = 256


GB = 4


def filter_kernel(idx_ref, cnt_ref, q_ref, r_ref, qt_ref, bias_ref, rtt_ref, col_ref, row_ref,
                  c_scr, h_scr, rt_ref, f_scr):
    t = pl.program_id(0)
    rows = q_ref.shape[0]
    hid = rtt_ref.shape[0]
    cells = rtt_ref.shape[1]
    depth = q_ref.shape[1]
    nq = rows // cells
    r4 = CH // cells
    br = r4 // 2
    groups = col_ref.shape[2] // 2
    scale = math.sqrt(depth)
    per = hid // 4

    @pl.when(t == 0)
    def _():
        rt_ref[...] = jnp.zeros(rt_ref.shape, rt_ref.dtype)
        for k in range(hid):
            blockk = rtt_ref[k]
            for x in range(r4):
                rt_ref[k, x * cells:(x + 1) * cells, x * cells:(x + 1) * cells] = blockk

    qt = q_ref[...]
    for g in range(groups):
        @pl.when(g * GB < cnt_ref[t])
        def _():
            for slot in range(GB):
                blk_id = idx_ref[t, g * GB + slot]
                start = pl.multiple_of(blk_id * (br * cells), br * cells)
                corr = lax.dot_general(
                    qt, r_ref[pl.ds(start, br * cells), :], (((1,), (1,)), ((), ())),
                    preferred_element_type=jnp.float32,
                )
                c_scr[:, slot * br * cells:(slot + 1) * br * cells] = (corr / scale).astype(jnp.bfloat16)
            for p in range(nq):
                for c2 in range(2):
                    cc = c_scr[p * cells:(p + 1) * cells, c2 * CH:(c2 + 1) * CH]
                    for kg in range(hid // per):
                        hq = jnp.dot(
                            qt_ref[kg * per * cells:(kg + 1) * per * cells, :], cc,
                            preferred_element_type=jnp.float32,
                        )
                        hq = jnp.maximum(hq + bias_ref[kg * per * cells:(kg + 1) * per * cells, :], 0.0)
                        hq = hq.astype(jnp.bfloat16)
                        for kk in range(per):
                            k = kg * per + kk
                            row0 = (p * 2 + c2) * cells
                            h_scr[k, row0:row0 + cells, :] = hq[kk * cells:(kk + 1) * cells, :]
            f_scr[...] = jnp.dot(h_scr[0], rt_ref[0], preferred_element_type=jnp.float32)
            for k in range(1, hid):
                f_scr[...] += jnp.dot(h_scr[k], rt_ref[k], preferred_element_type=jnp.float32)
            for p in range(nq):
                acc = f_scr[p * 2 * cells:(p + 1) * 2 * cells, :]
                col_ref[0, p, 2 * g:2 * g + 2, :] = jnp.max(acc.reshape(2, cells, CH), axis=1)
                accT = acc.T
                row_ref[0, p, :, 2 * g * cells:(2 * g + 2) * cells] = jnp.max(
                    accT.reshape(r4, cells, 2 * cells), axis=1)


def local_scores(q_all, r_all, cand, query_table, ref_table, tap_bias):
    tiles = q_all.shape[0]
    depth = q_all.shape[2]
    nrl, cells = r_all.shape[0], r_all.shape[1]
    hid = query_table.shape[0]
    qt_per = 4
    nb = cand.shape[1]
    br = nrl // nb
    chunks = nrl * cells // CH
    r4 = CH // cells
    keep = (cand != 0).astype(jnp.int32)
    idx = jnp.argsort(1 - keep, axis=1, stable=True).astype(jnp.int32)
    cnt = jnp.sum(keep, axis=1).astype(jnp.int32)
    qstack = query_table.reshape(hid * cells, cells)
    bias_col = jnp.repeat(tap_bias.astype(jnp.float32), cells)[:, None]
    rtT = jnp.transpose(ref_table, (0, 2, 1))
    r2 = r_all.reshape(nrl * cells, depth)
    col, row = pl.pallas_call(
        filter_kernel,
        grid_spec=pltpu.PrefetchScalarGridSpec(
            num_scalar_prefetch=2,
            grid=(tiles,),
            in_specs=[
                pl.BlockSpec((None, qt_per * cells, depth), lambda t, i, c: (t, 0, 0)),
                pl.BlockSpec((nrl * cells, depth), lambda t, i, c: (0, 0)),
                pl.BlockSpec((hid * cells, cells), lambda t, i, c: (0, 0)),
                pl.BlockSpec((hid * cells, 1), lambda t, i, c: (0, 0)),
                pl.BlockSpec((hid, cells, cells), lambda t, i, c: (0, 0, 0)),
            ],
            out_specs=[
                pl.BlockSpec((1, qt_per, chunks, CH), lambda t, i, c: (t, 0, 0, 0)),
                pl.BlockSpec((1, qt_per, r4, chunks * cells), lambda t, i, c: (t, 0, 0, 0)),
            ],
            scratch_shapes=[
                pltpu.VMEM((qt_per * cells, GB * br * cells), jnp.bfloat16),
                pltpu.VMEM((hid, qt_per * 2 * cells, CH), jnp.bfloat16),
                pltpu.VMEM((hid, CH, CH), jnp.bfloat16),
                pltpu.VMEM((qt_per * 2 * cells, CH), jnp.float32),
            ],
        ),
        out_shape=[
            jax.ShapeDtypeStruct((tiles, qt_per, chunks, CH), jnp.float32),
            jax.ShapeDtypeStruct((tiles, qt_per, r4, chunks * cells), jnp.float32),
        ],
        compiler_params=pltpu.CompilerParams(vmem_limit_bytes=56 * 1024 * 1024),
    )(idx, cnt, q_all, r2, qstack, bias_col, rtT)
    hi = lax.Precision.HIGHEST
    avg_c = (jnp.arange(CH)[:, None] // cells == jnp.arange(r4)[None, :]).astype(jnp.float32) / cells
    col_pool = jnp.einsum("tpcl,lr->tpcr", col, avg_c, precision=hi)
    avg_r = (jnp.arange(chunks * cells)[:, None] // cells == jnp.arange(chunks)[None, :]).astype(
        jnp.float32) / cells
    row_pool = jnp.einsum("tprl,lc->tpcr", row, avg_r, precision=hi)
    packed = (0.5 * (row_pool + col_pool)).reshape(tiles, qt_per, nb, br)
    where_is = jnp.argsort(idx, axis=1)
    return jnp.take_along_axis(packed, where_is[:, None, :, None], axis=2)


def doubling(x, axis, size):
    bits = size.bit_length() - 1
    for m in reversed(range(bits)):
        other = lax.ppermute(x, axis, [(i, i ^ (1 << m)) for i in range(size)])
        x = jnp.concatenate([x, other], axis=0)
    return x


def bit_reverse(size):
    bits = size.bit_length() - 1
    pos = jnp.arange(size)
    rev = jnp.zeros_like(pos)
    for i in range(bits):
        rev = rev | (((pos >> i) & 1) << (bits - 1 - i))
    return rev


def shards(queries, references, query_taps, ref_taps, tap_bias, candidates):
    query_table = conv_table(query_taps, SIDE)
    ref_table = conv_table(ref_taps, SIDE)
    blk = lax.axis_size("blk")
    wide = lax.axis_size("wide")
    me = lax.axis_index("blk")
    me_w = lax.axis_index("wide")
    query_unit = normalize(queries)
    qt_per, cells, depth = query_unit.shape
    pad = 16
    cand_rows = jnp.zeros((pad, depth), jnp.bfloat16).at[0, :candidates.shape[1]].set(
        candidates[0].astype(jnp.bfloat16))
    payload = jnp.concatenate([query_unit.reshape(qt_per * cells, depth), cand_rows], axis=0)
    q3 = doubling(payload[None], "blk", blk)
    cand = q3[:, qt_per * cells, :candidates.shape[1]]
    b_at = me ^ bit_reverse(blk)
    ref_unit = normalize(references)
    rl = ref_unit.shape[0]
    held = doubling(ref_unit, "wide", wide)
    w_at = me_w ^ bit_reverse(wide)
    cand_pos = jnp.take(cand, w_at, axis=1)
    s = local_scores(q3, held, cand_pos, query_table, ref_table, tap_bias)
    p_of = jnp.argsort(w_at)
    s = jnp.take(s, p_of, axis=2)
    s = jnp.take(s, jnp.argsort(b_at), axis=0)
    mine = lax.all_to_all(s, "blk", 0, 0, tiled=True)
    mine = jnp.transpose(mine, (1, 2, 0, 3)).reshape(qt_per, wide * blk * rl)
    block_refs = blk * rl
    keep = jnp.repeat(candidates[0] != 0, block_refs)
    return jnp.where(keep[None, :], mine, jnp.float32(0.0))


def solution(mesh):
    placed = (
        P(("wide", "blk"), None, None),
        P(("wide", "blk"), None, None),
        P(),
        P(),
        P(),
        P(("wide", "blk"), None),
    )
    return jax.shard_map(
        shards, mesh=mesh, in_specs=placed, out_specs=P(("wide", "blk"), None), check_vma=False
    )
```
